32 devices in a mesh: inline: 4 (over x, core), xline: 8 (over z, y).
Axes of the slice: x: 2, y: 2, z: 4, core: 2. Of those that a mesh axis runs over, the one named last changes fastest.
Arguments:
- image: bfloat16 [128, 512, 1024], P('inline', 'xline'), may hold values from -6 to 6
- weights: bfloat16 [4, 8, 2048, 1024], P('inline', 'xline'), may hold values from -0.1875 to 0.1875
- observed: bfloat16 [4096, 2048], P(('inline', 'xline')), may hold values from -6 to 6
- wavelet: float32 [33], replicated, may hold values from -0.375 to 0.375
- taps: float32 [9], replicated, may hold values from 0.1 to 0.6
- aperture: int32 [512, 8], P(('inline', 'xline')), may hold values from 0 to 31, all different within a row; in each aligned block of 16 rows (0 to 15, 16 to 31, ...) at most 8 rows name the same one
- landing: int32 [4096, 8], P(('inline', 'xline')), may hold values from 0 to 2047
Outputs:
- gradient: float32 [128, 512, 1024], P('inline', 'xline')
- residual: float32 [4096, 2048], P(('inline', 'xline'))
The draws below stay inside these ranges and needn't reach their ends.
Inputs may be any that keep to these rules, and one draw needn't show every extreme that they name: `aperture`: each row names 8 different tiles; within the 16 rows of one device no tile is named more than 8 times, a bound that some block reaches. Tile i * 8 + j is the image tile of inline index i and crossline index j. `landing`: A column index a * 64 + b within a tile.
All inputs are finite; a program needn't handle non-finite values.
Results may differ from the reference program's by a relative error of at most 0.0035.
Values may be sent and summed in bfloat16 or wider, within the bound.
No kernel may reach another device: no remote copies, remote signals or barrier semaphores. Data moves between devices by JAX's collectives and lax.ppermute only.
A program may use at most 128 MiB of HBM per device.

```python
import math
import jax
import jax.numpy as jnp
import numpy as np
from jax import lax

DEPTH = 1024
NS = 2048
CX = 32
CY = 64
BLK_DEV = 16
TB = 8
APER = 8
WL = 33
SMOOTH = 9
CAP = 8
NXI = 128
NYI = 512
BLOCKS = 512
TRACES = 4096
N_INLINE = 4
N_XLINE = 8
DEVICES = 32


def set_ends(values, stream_key, smallest, top_value):
    extent = values.shape
    index_at = [jax.random.randint(jax.random.fold_in(stream_key, axis), (), 0, extent[axis]) for axis in range(len(extent))]
    values = values.at[tuple(index_at)].set(smallest)
    longest = extent.index(max(extent))
    index_at[longest] = (index_at[longest] + 1) % extent[longest]
    return values.at[tuple(index_at)].set(top_value)


def block_levels(stream_key, extent, cuts, low, top_value):
    def one(axis_at, blocks):
        steps = jax.random.uniform(jax.random.fold_in(jax.random.fold_in(stream_key, 6), axis_at), (blocks,), jnp.float32, low / len(cuts), top_value / len(cuts))
        return jnp.repeat(jnp.exp(steps), extent[axis_at] // blocks).reshape((-1,) + (1,) * (len(extent) - axis_at - 1))

    loudness = one(*cuts[0])
    for cut in cuts[1:]:
        loudness = loudness * one(*cut)
    return loudness


def routed_block(stream_key, own, number, rows, amount, top, limit, slope):
    ranking = jax.random.permutation(stream_key, amount)
    packed, ordinary = load_shares(amount, rows * top, limit, slope, True), load_shares(amount, rows * top, limit, slope, False)
    places = jnp.arange(amount)

    def named(sizes, offset_by):
        used = int((sizes > 0).sum())
        fixed = max(1, used // 4)
        shifted = fixed + (places - fixed + offset_by * (used - fixed)) % max(1, amount - fixed)
        return jnp.zeros((amount,), jnp.int32).at[ranking[jnp.where(places < fixed, places, shifted)]].set(jnp.asarray(sizes, jnp.int32))

    sizes = jnp.where(number % 4 == 0, named(packed, number // 4), named(ordinary, number - number // 4 - 1))
    mixed = jax.random.permutation(jax.random.fold_in(own, 3), amount)
    giver, taker = mixed[0:amount // 2 * 2:2], mixed[1:amount // 2 * 2:2]
    slack = jnp.minimum(sizes[giver] - 1, limit - sizes[taker]) // 2
    slack = jnp.where((giver == ranking[0]) | (taker == ranking[0]) | (sizes[taker] == 0), 0, jnp.maximum(slack, 0))
    shifted = jax.random.randint(jax.random.fold_in(own, 4), (amount // 2,), 0, 1 << 20) % (slack + 1)
    sizes = sizes.at[giver].add(-shifted).at[taker].add(shifted)
    items = jnp.searchsorted(jnp.cumsum(sizes), jnp.arange(rows * top), side="right").astype(jnp.int32)
    grid = items.reshape(top, rows).T
    grid = grid[jax.random.permutation(jax.random.fold_in(own, 1), rows)]
    offset_by = jax.random.randint(jax.random.fold_in(own, 2), (rows, 1), 0, top)
    return jnp.take_along_axis(grid, (jnp.arange(top)[None, :] + offset_by) % top, axis=1)


def load_shares(count, total, reach, lean, full):
    weights = [(1 << 20) // math.isqrt(grade ** lean) + 1 for grade in range(1, count + 1)]
    largest = reach if full else min(reach, max(-(-total // count), total * weights[0] // sum(weights)))
    least = 1 if total - largest >= count - 1 else 0
    given, spare = [largest] + [least] * (count - 1), total - largest - least * (count - 1)
    while spare > 0:
        free = [i for i in range(1, count) if given[i] < largest] or [i for i in range(1, count) if given[i] < reach]
        pool, remaining = sum([weights[i] for i in free]), spare
        for i in free:
            addition = min(reach - given[i], max(1, remaining * weights[i] // pool), spare)
            given[i] = given[i] + addition
            spare = spare - addition
    return np.array(given)


def scatter_about(own_key, dims, width, bound, split=(), held_as=jnp.bfloat16):
    drawn = jax.random.normal(own_key, dims, jnp.float32) * width
    if len(split) > 0:
        drawn = block_levels(own_key, dims, split, -0.22, 0.18) * drawn
    return jnp.clip(drawn, min=-bound, max=bound).astype(held_as)


def setup_inputs(seed: int = 0) -> dict:
    keys = jax.random.split(jax.random.key(seed), 8)
    image = scatter_about(keys[0], (NXI, NYI, DEPTH), 1.0, 6.0, ((0, 4), (1, 8)))
    weights = scatter_about(keys[1], (N_INLINE, N_XLINE, NS, DEPTH), DEPTH ** -0.5, 0.1875, ((0, 4), (1, 8)))
    observed = scatter_about(keys[2], (TRACES, NS), 1.0, 6.0, ((0, 32),))
    wavelet = scatter_about(keys[3], (WL,), 0.06, 0.375, (), jnp.float32)
    taps = jnp.clip(jax.random.uniform(keys[4], (SMOOTH,), jnp.float32, 0.1, 0.6), 0.1, 0.6)
    aperture_keys = jax.random.split(jax.random.fold_in(keys[5], 1), BLOCKS // BLK_DEV)
    aperture_turns = jax.random.permutation(jax.random.fold_in(keys[5], 3), BLOCKS // BLK_DEV)
    aperture = jax.vmap(lambda own, number: routed_block(jax.random.fold_in(keys[5], 2), own, number, BLK_DEV, DEVICES, APER, CAP, 2))(aperture_keys, aperture_turns).reshape((BLOCKS, APER))
    landing = set_ends(jax.random.randint(keys[6], (TRACES, APER), 0, CX * CY), jax.random.fold_in(keys[6], 1), 0, (CX * CY) - 1).astype(jnp.int32)
    return {"image": image, "weights": weights, "observed": observed, "wavelet": wavelet, "taps": taps, "aperture": aperture, "landing": landing}


def convolve(signal, wavelet):
    pad_width = WL // 2
    padded = jnp.pad(signal, ((0, 0), (pad_width, pad_width)))
    length = signal.shape[1]
    result = jnp.zeros_like(signal)
    for offset in range(WL):
        start = 2 * pad_width - offset
        result = result + wavelet[offset] * padded[:, start:start + length]
    return result


def correlate(signal, wavelet):
    pad_width = WL // 2
    padded = jnp.pad(signal, ((0, 0), (pad_width, pad_width)))
    length = signal.shape[1]
    result = jnp.zeros_like(signal)
    for offset in range(WL):
        result = result + wavelet[offset] * padded[:, offset:offset + length]
    return result


def smooth_axis(field, taps, axis):
    length = field.shape[axis]
    widths = [(0, 0)] * field.ndim
    widths[axis] = (4, 4)
    padded = jnp.pad(field, widths)
    result = jnp.zeros_like(field)
    for offset in range(9):
        result = result + taps[offset] * lax.slice_in_dim(padded, offset, offset + length, axis=axis)
    return result


def reference(image, weights, observed, wavelet, taps, aperture, landing):
    device_count = N_INLINE * N_XLINE
    cell_count = CX * CY
    tiles = image.reshape(N_INLINE, CX, N_XLINE, CY, DEPTH).transpose(0, 2, 1, 3, 4).reshape(device_count, cell_count, DEPTH)
    weight_tiles = weights.reshape(device_count, NS, DEPTH)

    def forward_tile(pair):
        table = lax.dot_general(pair[0], pair[1], (((1,), (1,)), ((), ())), preferred_element_type=jnp.float32)
        return table.astype(jnp.bfloat16)

    tile_table = lax.map(forward_tile, (tiles, weight_tiles))
    target_tile = jnp.repeat(aperture, TB, axis=0)
    synthetic = jnp.zeros((TRACES, NS), jnp.float32)
    for entry in range(APER):
        part_value = tile_table[target_tile[:, entry], landing[:, entry]]
        synthetic = synthetic + part_value.astype(jnp.float32)
    modeled = convolve(synthetic, wavelet)
    residual = modeled - observed.astype(jnp.float32)
    adjoint = correlate(residual, wavelet).astype(jnp.bfloat16)
    adjoint_wide = lax.optimization_barrier(adjoint).astype(jnp.float32)
    gathered = jnp.zeros((device_count, cell_count, NS), jnp.float32)
    for entry in range(APER):
        gathered = gathered.at[target_tile[:, entry], landing[:, entry]].add(adjoint_wide)

    def adjoint_tile(pair):
        return jnp.dot(pair[0], pair[1].astype(jnp.float32), precision=lax.Precision.HIGHEST)

    raw_tiles = lax.map(adjoint_tile, (gathered, weight_tiles))
    raw_grid = raw_tiles.reshape(N_INLINE, N_XLINE, CX, CY, DEPTH).transpose(0, 2, 1, 3, 4).reshape(NXI, NYI, DEPTH)
    smooth_z = smooth_axis(raw_grid, taps, 2)
    smooth_x = smooth_axis(smooth_z, taps, 0)
    gradient = smooth_axis(smooth_x, taps, 1)
    return gradient, residual
```

```python
import jax
import jax.numpy as jnp
from jax import lax
from jax.sharding import PartitionSpec as P

CHUNK = 128
HALO = 64


def extended(block, sides, width):
    for axis, dim in sides:
        count = lax.axis_size(axis)
        forward = [(i, i + 1) for i in range(count - 1)]
        backward = [(target, source) for source, target in forward]
        low = lax.ppermute(
            lax.slice_in_dim(block, block.shape[dim] - width, None, axis=dim), axis, forward
        )
        high = lax.ppermute(lax.slice_in_dim(block, 0, width, axis=dim), axis, backward)
        block = jnp.concatenate([low, block, high], axis=dim)
    return block


def toeplitz_block(wavelet, sign):
    half = wavelet.shape[0] // 2
    k = jnp.arange(CHUNK + 2 * HALO)[:, None]
    n = jnp.arange(CHUNK)[None, :]
    if sign > 0:
        tap = n - k + HALO + half
    else:
        tap = k - n - HALO + half
    block = jnp.zeros((CHUNK + 2 * HALO, CHUNK), jnp.float32)
    for j in range(wavelet.shape[0]):
        block = jnp.where(tap == j, wavelet[j], block)
    return block


def banded(signal, block):
    rows, length = signal.shape
    chunks = length // CHUNK
    padded = jnp.pad(signal, ((0, 0), (HALO, HALO)))
    pieces = padded.reshape(rows, chunks + 1, CHUNK)
    windows = jnp.concatenate([pieces[:, :chunks], pieces[:, 1:]], axis=-1)
    out = jnp.einsum(
        "tok,kn->ton", windows, block, precision=lax.Precision.HIGHEST,
        preferred_element_type=jnp.float32,
    )
    return out.reshape(rows, length)


def filter_padded(padded, taps, axis):
    length = padded.shape[axis] - 8
    shape_out = list(padded.shape)
    shape_out[axis] = length
    result = jnp.zeros(tuple(shape_out), jnp.float32)
    for offset in range(9):
        result = result + taps[offset] * lax.slice_in_dim(
            padded, offset, offset + length, axis=axis
        )
    return result


def traverse(blocks):
    return lax.all_to_all(blocks, ("inline", "xline"), split_axis=0, concat_axis=0, tiled=True)


def local(image, weights, observed, wavelet, taps, aperture, landing):
    axes = ("inline", "xline")
    device_count = lax.axis_size("inline") * lax.axis_size("xline")
    me = lax.axis_index("inline") * lax.axis_size("xline") + lax.axis_index("xline")
    block_count, aperture_len = aperture.shape
    trace_count, samples = observed.shape
    per_block = trace_count // block_count
    rows_x, rows_y, depth_len = image.shape
    cell_count = rows_x * rows_y
    capacity = 2 * max(1, block_count * aperture_len // device_count)
    item_count = block_count * aperture_len
    target_tile = aperture.reshape(item_count)
    onehot = (target_tile[:, None] == jnp.arange(device_count, dtype=jnp.int32)[None, :]).astype(
        jnp.int32
    )
    before = jnp.cumsum(onehot, axis=0) - onehot
    slot_index = jnp.sum(before * onehot, axis=1)
    target_slot = target_tile * capacity + slot_index
    item_cells = (
        landing.reshape(block_count, per_block, aperture_len)
        .transpose(0, 2, 1)
        .reshape(item_count, per_block)
    )
    cell_send = (
        jnp.zeros((device_count * capacity, per_block), jnp.int32).at[target_slot].set(item_cells)
    )
    cell_recv = lax.all_to_all(
        cell_send.reshape(device_count, capacity * per_block),
        axes,
        split_axis=0,
        concat_axis=0,
        tiled=True,
    )
    cell_recv = cell_recv.reshape(device_count * capacity * per_block)
    tile_rows = image.reshape(cell_count, depth_len)
    weight_matrix = weights.reshape(samples, depth_len)
    contract = (((1,), (1,)), ((), ()))
    tile_table = lax.dot_general(
        tile_rows, weight_matrix, contract, preferred_element_type=jnp.float32
    )
    predicted = jnp.take(tile_table.astype(jnp.bfloat16), cell_recv, axis=0)
    outgoing = predicted.reshape(device_count, capacity * per_block, samples)
    returned = traverse(outgoing).reshape(device_count * capacity, per_block, samples)
    own_preds = jnp.take(returned, target_slot, axis=0).reshape(
        block_count, aperture_len, per_block, samples
    )
    synthetic = jnp.sum(own_preds.astype(jnp.float32), axis=1).reshape(trace_count, samples)
    modeled = banded(synthetic, toeplitz_block(wavelet, 1))
    residual = modeled - observed.astype(jnp.float32)
    adjoint = banded(residual, toeplitz_block(wavelet, -1)).astype(jnp.bfloat16)

    adjoint_all = lax.all_gather(adjoint, axes, axis=0, tiled=True)
    aperture_all = lax.all_gather(aperture, axes, axis=0, tiled=True)
    landing_all = lax.all_gather(landing, axes, axis=0, tiled=True)
    all_blocks = aperture_all.shape[0]
    relevant = capacity * device_count
    hit = aperture_all == me
    has = jnp.any(hit, axis=1)
    entry = jnp.argmax(hit, axis=1).astype(jnp.int32)
    position = jnp.cumsum(has.astype(jnp.int32)) - 1
    slot = jnp.where(has, position, relevant)
    chosen = (
        jnp.zeros((relevant,), jnp.int32)
        .at[slot]
        .set(jnp.arange(all_blocks, dtype=jnp.int32), mode="drop")
    )
    found = jnp.sum(has.astype(jnp.int32))
    cells_all = jnp.take_along_axis(
        landing_all.reshape(all_blocks, per_block, aperture_len), entry[:, None, None], axis=2
    )[:, :, 0]
    cells = jnp.where(
        (jnp.arange(relevant) < found)[:, None], jnp.take(cells_all, chosen, axis=0), cell_count
    )
    picked = jnp.take(adjoint_all.reshape(all_blocks, per_block, samples), chosen, axis=0)
    per_trace = jnp.dot(
        picked.reshape(relevant * per_block, samples),
        weight_matrix,
        preferred_element_type=jnp.float32,
    )
    raw_gradient = (
        jnp.zeros((cell_count, depth_len), jnp.float32)
        .at[cells.reshape(relevant * per_block)]
        .add(per_trace, mode="drop")
    )
    raw_gradient = raw_gradient.reshape(rows_x, rows_y, depth_len)
    depth_padded = jnp.pad(raw_gradient, ((0, 0), (0, 0), (4, 4)))
    smooth_z = filter_padded(depth_padded, taps, 2)
    inline_wide = extended(smooth_z, (("inline", 0),), 4)
    smooth_x = filter_padded(inline_wide, taps, 0)
    xline_wide = extended(smooth_x, (("xline", 1),), 4)
    gradient = filter_padded(xline_wide, taps, 1)
    return (gradient, residual)


def solution(mesh):
    return jax.shard_map(
        local,
        mesh=mesh,
        in_specs=(
            P("inline", "xline", None),
            P("inline", "xline", None, None),
            P(("inline", "xline"), None),
            P(),
            P(),
            P(("inline", "xline"), None),
            P(("inline", "xline"), None),
        ),
        out_specs=(P("inline", "xline", None), P(("inline", "xline"), None)),
        check_vma=False,
    )
```

```python
import jax
import jax.numpy as jnp
from jax import lax
from jax.sharding import PartitionSpec as P

CHUNK = 128
HALO = 64


def extended(block, sides, width):
    for axis, dim in sides:
        count = lax.axis_size(axis)
        forward = [(i, i + 1) for i in range(count - 1)]
        backward = [(target, source) for source, target in forward]
        low = lax.ppermute(
            lax.slice_in_dim(block, block.shape[dim] - width, None, axis=dim), axis, forward
        )
        high = lax.ppermute(lax.slice_in_dim(block, 0, width, axis=dim), axis, backward)
        block = jnp.concatenate([low, block, high], axis=dim)
    return block


def band_block(values, centre):
    k = jnp.arange(CHUNK + 2 * HALO)[:, None]
    n = jnp.arange(CHUNK)[None, :]
    tap = k - n - HALO + centre
    block = jnp.zeros((CHUNK + 2 * HALO, CHUNK), jnp.float32)
    for j in range(values.shape[0]):
        block = jnp.where(tap == j, values[j], block)
    return block


def split(x):
    high = lax.reduce_precision(x, exponent_bits=8, mantissa_bits=7)
    return high.astype(jnp.bfloat16), (x - high).astype(jnp.bfloat16)


def windows(x):
    rows, length = x.shape
    chunks = length // CHUNK
    padded = jnp.pad(x, ((0, 0), (HALO, HALO)))
    pieces = padded.reshape(rows, chunks + 1, CHUNK)
    joined = jnp.concatenate([pieces[:, :chunks], pieces[:, 1:]], axis=-1)
    return joined.reshape(rows * chunks, CHUNK + 2 * HALO)


def banded(signal, block):
    rows, length = signal.shape
    x_high, x_low = split(signal)
    b_high, b_low = split(block)
    w_high, w_low = windows(x_high), windows(x_low)
    out = (
        jnp.dot(w_high, b_high, preferred_element_type=jnp.float32)
        + jnp.dot(w_high, b_low, preferred_element_type=jnp.float32)
        + jnp.dot(w_low, b_high, preferred_element_type=jnp.float32)
    )
    return out.reshape(rows, length)


def filter_padded(padded, taps, axis):
    length = padded.shape[axis] - 8
    shape_out = list(padded.shape)
    shape_out[axis] = length
    result = jnp.zeros(tuple(shape_out), jnp.float32)
    for offset in range(9):
        result = result + taps[offset] * lax.slice_in_dim(
            padded, offset, offset + length, axis=axis
        )
    return result


def traverse(blocks):
    return lax.all_to_all(blocks, ("inline", "xline"), split_axis=0, concat_axis=0, tiled=True)


def local(image, weights, observed, wavelet, taps, aperture, landing):
    axes = ("inline", "xline")
    device_count = lax.axis_size("inline") * lax.axis_size("xline")
    me = lax.axis_index("inline") * lax.axis_size("xline") + lax.axis_index("xline")
    block_count, aperture_len = aperture.shape
    trace_count, samples = observed.shape
    per_block = trace_count // block_count
    rows_x, rows_y, depth_len = image.shape
    cell_count = rows_x * rows_y
    capacity = 2 * max(1, block_count * aperture_len // device_count)
    item_count = block_count * aperture_len
    tables = jnp.concatenate(
        [aperture, landing.reshape(block_count, per_block * aperture_len)], axis=1
    ).astype(jnp.float32)
    tables_all = jnp.round(lax.all_gather(tables, axes, axis=0, tiled=True))
    target_tile = aperture.reshape(item_count)
    onehot = (target_tile[:, None] == jnp.arange(device_count, dtype=jnp.int32)[None, :]).astype(
        jnp.int32
    )
    before = jnp.cumsum(onehot, axis=0) - onehot
    slot_index = jnp.sum(before * onehot, axis=1)
    target_slot = target_tile * capacity + slot_index
    item_cells = (
        landing.reshape(block_count, per_block, aperture_len)
        .transpose(0, 2, 1)
        .reshape(item_count, per_block)
    )
    cell_send = (
        jnp.zeros((device_count * capacity, per_block), jnp.int32).at[target_slot].set(item_cells)
    )
    cell_recv = lax.all_to_all(
        cell_send.reshape(device_count, capacity * per_block),
        axes,
        split_axis=0,
        concat_axis=0,
        tiled=True,
    )
    cell_recv = cell_recv.reshape(device_count * capacity * per_block)
    tile_rows = image.reshape(cell_count, depth_len)
    weight_matrix = weights.reshape(samples, depth_len)
    contract = (((1,), (1,)), ((), ()))
    tile_table = lax.dot_general(
        tile_rows, weight_matrix, contract, preferred_element_type=jnp.float32
    )
    predicted = jnp.take(tile_table.astype(jnp.bfloat16), cell_recv, axis=0)
    outgoing = predicted.reshape(device_count, capacity * per_block, samples)
    returned = traverse(outgoing).reshape(device_count * capacity, per_block, samples)
    own_preds = jnp.take(returned, target_slot, axis=0).reshape(
        block_count, aperture_len, per_block, samples
    )
    synthetic = jnp.sum(own_preds.astype(jnp.float32), axis=1).reshape(trace_count, samples)
    half = wavelet.shape[0] // 2
    modeled = banded(synthetic, band_block(wavelet[::-1], half))
    residual = modeled - observed.astype(jnp.float32)
    adjoint = banded(residual, band_block(wavelet, half)).astype(jnp.bfloat16)

    adjoint_all = lax.all_gather(adjoint, axes, axis=0, tiled=True)
    all_blocks = block_count * device_count
    aperture_all = tables_all[:, :aperture_len].astype(jnp.int32)
    landing_all = tables_all[:, aperture_len:].astype(jnp.int32).reshape(all_blocks * per_block, aperture_len)
    relevant = capacity * device_count
    hit = aperture_all == me
    has = jnp.any(hit, axis=1)
    entry = jnp.argmax(hit, axis=1).astype(jnp.int32)
    position = jnp.cumsum(has.astype(jnp.int32)) - 1
    slot = jnp.where(has, position, relevant)
    chosen = (
        jnp.zeros((relevant,), jnp.int32)
        .at[slot]
        .set(jnp.arange(all_blocks, dtype=jnp.int32), mode="drop")
    )
    found = jnp.sum(has.astype(jnp.int32))
    cells_all = jnp.take_along_axis(
        landing_all.reshape(all_blocks, per_block, aperture_len), entry[:, None, None], axis=2
    )[:, :, 0]
    cells = jnp.where(
        (jnp.arange(relevant) < found)[:, None], jnp.take(cells_all, chosen, axis=0), cell_count
    )
    picked = jnp.take(adjoint_all.reshape(all_blocks, per_block, samples), chosen, axis=0)
    per_trace = jnp.dot(
        picked.reshape(relevant * per_block, samples),
        weight_matrix,
        preferred_element_type=jnp.float32,
    )
    raw_gradient = (
        jnp.zeros((cell_count, depth_len), jnp.float32)
        .at[cells.reshape(relevant * per_block)]
        .add(per_trace, mode="drop")
    )
    smooth_z = banded(raw_gradient, band_block(taps, taps.shape[0] // 2))
    smooth_z = smooth_z.reshape(rows_x, rows_y, depth_len)
    inline_wide = extended(smooth_z, (("inline", 0),), 4)
    smooth_x = filter_padded(inline_wide, taps, 0)
    xline_wide = extended(smooth_x, (("xline", 1),), 4)
    gradient = filter_padded(xline_wide, taps, 1)
    return (gradient, residual)


def solution(mesh):
    return jax.shard_map(
        local,
        mesh=mesh,
        in_specs=(
            P("inline", "xline", None),
            P("inline", "xline", None, None),
            P(("inline", "xline"), None),
            P(),
            P(),
            P(("inline", "xline"), None),
            P(("inline", "xline"), None),
        ),
        out_specs=(P("inline", "xline", None), P(("inline", "xline"), None)),
        check_vma=False,
    )
```

```python
import jax
import jax.numpy as jnp
from jax import lax
from jax.sharding import PartitionSpec as P

CHUNK = 128
HALO = 64


def extended(block, sides, width):
    for axis, dim in sides:
        count = lax.axis_size(axis)
        forward = [(i, i + 1) for i in range(count - 1)]
        backward = [(target, source) for source, target in forward]
        low = lax.ppermute(
            lax.slice_in_dim(block, block.shape[dim] - width, None, axis=dim), axis, forward
        )
        high = lax.ppermute(lax.slice_in_dim(block, 0, width, axis=dim), axis, backward)
        block = jnp.concatenate([low, block, high], axis=dim)
    return block


def band_block(values, centre):
    k = jnp.arange(CHUNK + 2 * HALO)[:, None]
    n = jnp.arange(CHUNK)[None, :]
    tap = k - n - HALO + centre
    block = jnp.zeros((CHUNK + 2 * HALO, CHUNK), jnp.float32)
    for j in range(values.shape[0]):
        block = jnp.where(tap == j, values[j], block)
    return block


def split(x):
    high = lax.reduce_precision(x, exponent_bits=8, mantissa_bits=7)
    return high.astype(jnp.bfloat16), (x - high).astype(jnp.bfloat16)


def windows(x):
    rows, length = x.shape
    chunks = length // CHUNK
    padded = jnp.pad(x, ((0, 0), (HALO, HALO)))
    pieces = padded.reshape(rows, chunks + 1, CHUNK)
    joined = jnp.concatenate([pieces[:, :chunks], pieces[:, 1:]], axis=-1)
    return joined.reshape(rows * chunks, CHUNK + 2 * HALO)


def banded(signal, block):
    rows, length = signal.shape
    x_high, x_low = split(signal)
    b_high, b_low = lax.optimization_barrier(split(block))
    w_high, w_low = windows(x_high), windows(x_low)
    out = (
        jnp.dot(w_high, b_high, preferred_element_type=jnp.float32)
        + jnp.dot(w_high, b_low, preferred_element_type=jnp.float32)
        + jnp.dot(w_low, b_high, preferred_element_type=jnp.float32)
    )
    return out.reshape(rows, length)


def filter_padded(padded, taps, axis):
    length = padded.shape[axis] - 8
    shape_out = list(padded.shape)
    shape_out[axis] = length
    result = jnp.zeros(tuple(shape_out), jnp.float32)
    for offset in range(9):
        result = result + taps[offset] * lax.slice_in_dim(
            padded, offset, offset + length, axis=axis
        )
    return result


def traverse(blocks):
    return lax.all_to_all(blocks, ("inline", "xline"), split_axis=0, concat_axis=0, tiled=True)


def local(image, weights, observed, wavelet, taps, aperture, landing):
    axes = ("inline", "xline")
    device_count = lax.axis_size("inline") * lax.axis_size("xline")
    me = lax.axis_index("inline") * lax.axis_size("xline") + lax.axis_index("xline")
    block_count, aperture_len = aperture.shape
    trace_count, samples = observed.shape
    per_block = trace_count // block_count
    rows_x, rows_y, depth_len = image.shape
    cell_count = rows_x * rows_y
    capacity = 2 * max(1, block_count * aperture_len // device_count)
    item_count = block_count * aperture_len
    tables = jnp.concatenate(
        [aperture, landing.reshape(block_count, per_block * aperture_len)], axis=1
    ).astype(jnp.float32)
    tables_all = jnp.round(lax.all_gather(tables, axes, axis=0, tiled=True))
    target_tile = aperture.reshape(item_count)
    onehot = (target_tile[:, None] == jnp.arange(device_count, dtype=jnp.int32)[None, :]).astype(
        jnp.int32
    )
    before = jnp.cumsum(onehot, axis=0) - onehot
    slot_index = jnp.sum(before * onehot, axis=1)
    target_slot = target_tile * capacity + slot_index
    item_cells = (
        landing.reshape(block_count, per_block, aperture_len)
        .transpose(0, 2, 1)
        .reshape(item_count, per_block)
    )
    cell_send = (
        jnp.zeros((device_count * capacity, per_block), jnp.int32).at[target_slot].set(item_cells)
    )
    cell_recv = lax.all_to_all(
        cell_send.reshape(device_count, capacity * per_block),
        axes,
        split_axis=0,
        concat_axis=0,
        tiled=True,
    )
    cell_recv = cell_recv.reshape(device_count * capacity * per_block)
    tile_rows = image.reshape(cell_count, depth_len)
    weight_matrix = weights.reshape(samples, depth_len)
    contract = (((1,), (1,)), ((), ()))
    tile_table = lax.dot_general(
        tile_rows, weight_matrix, contract, preferred_element_type=jnp.float32
    )
    predicted = jnp.take(tile_table.astype(jnp.bfloat16), cell_recv, axis=0)
    outgoing = predicted.reshape(device_count, capacity * per_block, samples)
    returned = traverse(outgoing).reshape(device_count * capacity, per_block, samples)
    own_preds = jnp.take(returned, target_slot, axis=0).reshape(
        block_count, aperture_len, per_block, samples
    )
    synthetic = jnp.sum(own_preds.astype(jnp.float32), axis=1).reshape(trace_count, samples)
    half = wavelet.shape[0] // 2
    modeled = banded(synthetic, band_block(wavelet[::-1], half))
    residual = modeled - observed.astype(jnp.float32)
    adjoint = banded(residual, band_block(wavelet, half)).astype(jnp.bfloat16)

    adjoint_all = lax.all_gather(adjoint, axes, axis=0, tiled=True)
    all_blocks = block_count * device_count
    aperture_all = tables_all[:, :aperture_len].astype(jnp.int32)
    landing_all = tables_all[:, aperture_len:].astype(jnp.int32).reshape(all_blocks * per_block, aperture_len)
    relevant = capacity * device_count
    hit = aperture_all == me
    has = jnp.any(hit, axis=1)
    entry = jnp.argmax(hit, axis=1).astype(jnp.int32)
    position = jnp.cumsum(has.astype(jnp.int32)) - 1
    slot = jnp.where(has, position, relevant)
    chosen = (
        jnp.zeros((relevant,), jnp.int32)
        .at[slot]
        .set(jnp.arange(all_blocks, dtype=jnp.int32), mode="drop")
    )
    found = jnp.sum(has.astype(jnp.int32))
    cells_all = jnp.take_along_axis(
        landing_all.reshape(all_blocks, per_block, aperture_len), entry[:, None, None], axis=2
    )[:, :, 0]
    cells = jnp.where(
        (jnp.arange(relevant) < found)[:, None], jnp.take(cells_all, chosen, axis=0), cell_count
    )
    picked = jnp.take(adjoint_all.reshape(all_blocks, per_block, samples), chosen, axis=0)
    per_trace = jnp.dot(
        picked.reshape(relevant * per_block, samples),
        weight_matrix,
        preferred_element_type=jnp.float32,
    )
    raw_gradient = (
        jnp.zeros((cell_count, depth_len), jnp.float32)
        .at[cells.reshape(relevant * per_block)]
        .add(per_trace, mode="drop")
    )
    smooth_z = banded(raw_gradient, band_block(taps, taps.shape[0] // 2))
    smooth_z = smooth_z.reshape(rows_x, rows_y, depth_len)
    inline_wide = extended(smooth_z, (("inline", 0),), 4)
    smooth_x = filter_padded(inline_wide, taps, 0)
    xline_wide = extended(smooth_x, (("xline", 1),), 4)
    gradient = filter_padded(xline_wide, taps, 1)
    return (gradient, residual)


def solution(mesh):
    return jax.shard_map(
        local,
        mesh=mesh,
        in_specs=(
            P("inline", "xline", None),
            P("inline", "xline", None, None),
            P(("inline", "xline"), None),
            P(),
            P(),
            P(("inline", "xline"), None),
            P(("inline", "xline"), None),
        ),
        out_specs=(P("inline", "xline", None), P(("inline", "xline"), None)),
        check_vma=False,
    )
```

```python
import jax
import jax.numpy as jnp
from jax import lax
from jax.sharding import PartitionSpec as P

CHUNK = 128
HALO = 64


def extended(block, sides, width):
    for axis, dim in sides:
        count = lax.axis_size(axis)
        forward = [(i, i + 1) for i in range(count - 1)]
        backward = [(target, source) for source, target in forward]
        low = lax.ppermute(
            lax.slice_in_dim(block, block.shape[dim] - width, None, axis=dim), axis, forward
        )
        high = lax.ppermute(lax.slice_in_dim(block, 0, width, axis=dim), axis, backward)
        block = jnp.concatenate([low, block, high], axis=dim)
    return block


def band_block(values, centre):
    k = jnp.arange(CHUNK + 2 * HALO)[:, None]
    n = jnp.arange(CHUNK)[None, :]
    tap = k - n - HALO + centre
    block = jnp.zeros((CHUNK + 2 * HALO, CHUNK), jnp.float32)
    for j in range(values.shape[0]):
        block = jnp.where(tap == j, values[j], block)
    return block


def split(x):
    high = lax.reduce_precision(x, exponent_bits=8, mantissa_bits=7)
    return high.astype(jnp.bfloat16), (x - high).astype(jnp.bfloat16)


def windows(x):
    rows, length = x.shape
    chunks = length // CHUNK
    padded = jnp.pad(x, ((0, 0), (HALO, HALO)))
    pieces = padded.reshape(rows, chunks + 1, CHUNK)
    joined = jnp.concatenate([pieces[:, :chunks], pieces[:, 1:]], axis=-1)
    return joined.reshape(rows * chunks, CHUNK + 2 * HALO)


def banded(signal, block):
    rows, length = signal.shape
    x_high, x_low = split(signal)
    b_high, b_low = lax.optimization_barrier(split(block))
    w_high, w_low = windows(x_high), windows(x_low)
    out = (
        jnp.dot(w_high, b_high, preferred_element_type=jnp.float32)
        + jnp.dot(w_high, b_low, preferred_element_type=jnp.float32)
        + jnp.dot(w_low, b_high, preferred_element_type=jnp.float32)
    )
    return out.reshape(rows, length)


def filter_padded(padded, taps, axis):
    length = padded.shape[axis] - 8
    shape_out = list(padded.shape)
    shape_out[axis] = length
    result = jnp.zeros(tuple(shape_out), jnp.float32)
    for offset in range(9):
        result = result + taps[offset] * lax.slice_in_dim(
            padded, offset, offset + length, axis=axis
        )
    return result


def traverse(blocks):
    return lax.all_to_all(blocks, ("inline", "xline"), split_axis=0, concat_axis=0, tiled=True)


def local(image, weights, observed, wavelet, taps, aperture, landing):
    axes = ("inline", "xline")
    device_count = lax.axis_size("inline") * lax.axis_size("xline")
    me = lax.axis_index("inline") * lax.axis_size("xline") + lax.axis_index("xline")
    block_count, aperture_len = aperture.shape
    trace_count, samples = observed.shape
    per_block = trace_count // block_count
    rows_x, rows_y, depth_len = image.shape
    cell_count = rows_x * rows_y
    capacity = 2 * max(1, block_count * aperture_len // device_count)
    item_count = block_count * aperture_len
    tables = jnp.concatenate(
        [aperture, landing.reshape(block_count, per_block * aperture_len)], axis=1
    ).astype(jnp.float32)
    tables_all = jnp.round(lax.all_gather(tables, axes, axis=0, tiled=True))
    target_tile = aperture.reshape(item_count)
    onehot = (target_tile[:, None] == jnp.arange(device_count, dtype=jnp.int32)[None, :]).astype(
        jnp.int32
    )
    before = jnp.cumsum(onehot, axis=0) - onehot
    slot_index = jnp.sum(before * onehot, axis=1)
    target_slot = target_tile * capacity + slot_index
    item_cells = (
        landing.reshape(block_count, per_block, aperture_len)
        .transpose(0, 2, 1)
        .reshape(item_count, per_block)
    )
    cell_send = (
        jnp.zeros((device_count * capacity, per_block), jnp.int32).at[target_slot].set(item_cells)
    )
    cell_recv = lax.all_to_all(
        cell_send.reshape(device_count, capacity * per_block),
        axes,
        split_axis=0,
        concat_axis=0,
        tiled=True,
    )
    cell_recv = cell_recv.reshape(device_count * capacity * per_block)
    tile_rows = image.reshape(cell_count, depth_len)
    weight_matrix = weights.reshape(samples, depth_len)
    contract = (((1,), (1,)), ((), ()))
    tile_table = lax.dot_general(
        tile_rows, weight_matrix, contract, preferred_element_type=jnp.float32
    )
    predicted = jnp.take(tile_table.astype(jnp.bfloat16), cell_recv, axis=0)
    outgoing = predicted.reshape(device_count, capacity * per_block, samples)
    returned = traverse(outgoing).reshape(device_count * capacity, per_block, samples)
    own_preds = jnp.take(returned, target_slot, axis=0).reshape(
        block_count, aperture_len, per_block, samples
    )
    synthetic = jnp.sum(own_preds.astype(jnp.float32), axis=1).reshape(trace_count, samples)
    half = wavelet.shape[0] // 2
    modeled = banded(synthetic, band_block(wavelet[::-1], half))
    residual = modeled - observed.astype(jnp.float32)
    adjoint = banded(residual, band_block(wavelet, half)).astype(jnp.bfloat16)

    adjoint_all = lax.all_gather(adjoint, axes, axis=0, tiled=True)
    all_blocks = block_count * device_count
    aperture_all = tables_all[:, :aperture_len].astype(jnp.int32)
    landing_all = tables_all[:, aperture_len:].astype(jnp.int32).reshape(all_blocks * per_block, aperture_len)
    relevant = capacity * device_count
    hit = aperture_all == me
    has = jnp.any(hit, axis=1)
    entry = jnp.argmax(hit, axis=1).astype(jnp.int32)
    position = jnp.cumsum(has.astype(jnp.int32)) - 1
    slot = jnp.where(has, position, relevant)
    chosen = (
        jnp.zeros((relevant,), jnp.int32)
        .at[slot]
        .set(jnp.arange(all_blocks, dtype=jnp.int32), mode="drop")
    )
    found = jnp.sum(has.astype(jnp.int32))
    cells_all = jnp.take_along_axis(
        landing_all.reshape(all_blocks, per_block, aperture_len), entry[:, None, None], axis=2
    )[:, :, 0]
    cells = jnp.where(
        (jnp.arange(relevant) < found)[:, None], jnp.take(cells_all, chosen, axis=0), cell_count
    )
    picked = jnp.take(adjoint_all.reshape(all_blocks, per_block, samples), chosen, axis=0)
    per_trace = jnp.dot(
        picked.reshape(relevant * per_block, samples),
        weight_matrix,
        preferred_element_type=jnp.float32,
    )
    raw_gradient = (
        jnp.zeros((cell_count, depth_len), jnp.float32)
        .at[cells.reshape(relevant * per_block)]
        .add(per_trace, mode="drop")
    )
    raw_gradient = raw_gradient.reshape(rows_x, rows_y, depth_len)
    depth_padded = jnp.pad(raw_gradient, ((0, 0), (0, 0), (4, 4)))
    smooth_z = filter_padded(depth_padded, taps, 2)
    inline_wide = extended(smooth_z, (("inline", 0),), 4)
    smooth_x = filter_padded(inline_wide, taps, 0)
    xline_wide = extended(smooth_x, (("xline", 1),), 4)
    gradient = filter_padded(xline_wide, taps, 1)
    return (gradient, residual)


def solution(mesh):
    return jax.shard_map(
        local,
        mesh=mesh,
        in_specs=(
            P("inline", "xline", None),
            P("inline", "xline", None, None),
            P(("inline", "xline"), None),
            P(),
            P(),
            P(("inline", "xline"), None),
            P(("inline", "xline"), None),
        ),
        out_specs=(P("inline", "xline", None), P(("inline", "xline"), None)),
        check_vma=False,
    )
```

```python
import jax
import jax.numpy as jnp
from jax import lax
from jax.experimental import pallas as pl
from jax.experimental.pallas import tpu as pltpu
from jax.sharding import PartitionSpec as P

HW = 4


def _zx_kernel(taps_ref, main_ref, low_ref, high_ref, out_ref, ext_ref):
    nx = main_ref.shape[0]
    ext_ref[0:HW] = low_ref[...]
    ext_ref[HW:HW + nx] = main_ref[...]
    ext_ref[HW + nx:] = high_ref[...]
    depth = ext_ref.shape[2]
    x = ext_ref[...]
    lane = lax.broadcasted_iota(jnp.int32, x.shape, 2)
    acc = taps_ref[HW] * x
    for j in range(2 * HW + 1):
        if j == HW:
            continue
        shifted = pltpu.roll(x, (HW - j) % depth, 2)
        source = lane + (j - HW)
        keep = (source >= 0) & (source < depth)
        acc = acc + taps_ref[j] * jnp.where(keep, shifted, 0.0)
    ext_ref[...] = acc
    out = taps_ref[0] * ext_ref[0:nx]
    for j in range(1, 2 * HW + 1):
        out = out + taps_ref[j] * ext_ref[j:j + nx]
    out_ref[...] = out


def smooth_zx(raw, low, high, taps, ty=8):
    nx, ny, nz = raw.shape
    grid = (ny // ty,)
    return pl.pallas_call(
        _zx_kernel,
        grid=grid,
        in_specs=[
            pl.BlockSpec(memory_space=pltpu.SMEM),
            pl.BlockSpec((nx, ty, nz), lambda i: (0, i, 0)),
            pl.BlockSpec((HW, ty, nz), lambda i: (0, i, 0)),
            pl.BlockSpec((HW, ty, nz), lambda i: (0, i, 0)),
        ],
        out_specs=pl.BlockSpec((nx, ty, nz), lambda i: (0, i, 0)),
        out_shape=jax.ShapeDtypeStruct(raw.shape, jnp.float32),
        scratch_shapes=[pltpu.VMEM((nx + 2 * HW, ty, nz), jnp.float32)],
        cost_estimate=pl.CostEstimate(flops=40 * raw.size, transcendentals=0, bytes_accessed=int(raw.size * 8 * 1.25)),
    )(taps, raw, low, high)


def _y_kernel(taps_ref, main_ref, low_ref, high_ref, out_ref, ext_ref):
    ny = main_ref.shape[1]
    ext_ref[:, HW:2 * HW] = low_ref[...]
    ext_ref[:, 2 * HW:2 * HW + ny] = main_ref[...]
    ext_ref[:, 2 * HW + ny:3 * HW + ny] = high_ref[...]
    out = taps_ref[0] * ext_ref[:, pl.ds(HW, ny)]
    for j in range(1, 2 * HW + 1):
        out = out + taps_ref[j] * ext_ref[:, pl.ds(HW + j, ny)]
    out_ref[...] = out


def smooth_y(field, low, high, taps, tx=4):
    nx, ny, nz = field.shape
    grid = (nx // tx,)
    return pl.pallas_call(
        _y_kernel,
        grid=grid,
        in_specs=[
            pl.BlockSpec(memory_space=pltpu.SMEM),
            pl.BlockSpec((tx, ny, nz), lambda i: (i, 0, 0)),
            pl.BlockSpec((tx, HW, nz), lambda i: (i, 0, 0)),
            pl.BlockSpec((tx, HW, nz), lambda i: (i, 0, 0)),
        ],
        out_specs=pl.BlockSpec((tx, ny, nz), lambda i: (i, 0, 0)),
        out_shape=jax.ShapeDtypeStruct(field.shape, jnp.float32),
        scratch_shapes=[pltpu.VMEM((tx, ny + 4 * HW, nz), jnp.float32)],
        cost_estimate=pl.CostEstimate(flops=18 * field.size, transcendentals=0, bytes_accessed=int(field.size * 8 * 1.1)),
    )(taps, field, low, high)


CHUNK = 128
HALO = 64


def halos(block, axis, dim, width):
    count = lax.axis_size(axis)
    forward = [(i, i + 1) for i in range(count - 1)]
    backward = [(target, source) for source, target in forward]
    low = lax.ppermute(
        lax.slice_in_dim(block, block.shape[dim] - width, None, axis=dim), axis, forward
    )
    high = lax.ppermute(lax.slice_in_dim(block, 0, width, axis=dim), axis, backward)
    return low, high


def extended(block, sides, width):
    for axis, dim in sides:
        count = lax.axis_size(axis)
        forward = [(i, i + 1) for i in range(count - 1)]
        backward = [(target, source) for source, target in forward]
        low = lax.ppermute(
            lax.slice_in_dim(block, block.shape[dim] - width, None, axis=dim), axis, forward
        )
        high = lax.ppermute(lax.slice_in_dim(block, 0, width, axis=dim), axis, backward)
        block = jnp.concatenate([low, block, high], axis=dim)
    return block


def band_block(values, centre):
    k = jnp.arange(CHUNK + 2 * HALO)[:, None]
    n = jnp.arange(CHUNK)[None, :]
    tap = k - n - HALO + centre
    block = jnp.zeros((CHUNK + 2 * HALO, CHUNK), jnp.float32)
    for j in range(values.shape[0]):
        block = jnp.where(tap == j, values[j], block)
    return block


def split(x):
    high = lax.reduce_precision(x, exponent_bits=8, mantissa_bits=7)
    return high.astype(jnp.bfloat16), (x - high).astype(jnp.bfloat16)


def windows(x):
    rows, length = x.shape
    chunks = length // CHUNK
    padded = jnp.pad(x, ((0, 0), (HALO, HALO)))
    pieces = padded.reshape(rows, chunks + 1, CHUNK)
    joined = jnp.concatenate([pieces[:, :chunks], pieces[:, 1:]], axis=-1)
    return joined.reshape(rows * chunks, CHUNK + 2 * HALO)


def banded(signal, block):
    rows, length = signal.shape
    x_high, x_low = split(signal)
    b_high, b_low = lax.optimization_barrier(split(block))
    w_high, w_low = windows(x_high), windows(x_low)
    out = (
        jnp.dot(w_high, b_high, preferred_element_type=jnp.float32)
        + jnp.dot(w_high, b_low, preferred_element_type=jnp.float32)
        + jnp.dot(w_low, b_high, preferred_element_type=jnp.float32)
    )
    return out.reshape(rows, length)


def filter_padded(padded, taps, axis):
    length = padded.shape[axis] - 8
    shape_out = list(padded.shape)
    shape_out[axis] = length
    result = jnp.zeros(tuple(shape_out), jnp.float32)
    for offset in range(9):
        result = result + taps[offset] * lax.slice_in_dim(
            padded, offset, offset + length, axis=axis
        )
    return result


def traverse(blocks):
    return lax.all_to_all(blocks, ("inline", "xline"), split_axis=0, concat_axis=0, tiled=True)


def local(image, weights, observed, wavelet, taps, aperture, landing):
    axes = ("inline", "xline")
    device_count = lax.axis_size("inline") * lax.axis_size("xline")
    me = lax.axis_index("inline") * lax.axis_size("xline") + lax.axis_index("xline")
    block_count, aperture_len = aperture.shape
    trace_count, samples = observed.shape
    per_block = trace_count // block_count
    rows_x, rows_y, depth_len = image.shape
    cell_count = rows_x * rows_y
    capacity = 2 * max(1, block_count * aperture_len // device_count)
    item_count = block_count * aperture_len
    tables = jnp.concatenate(
        [aperture, landing.reshape(block_count, per_block * aperture_len)], axis=1
    ).astype(jnp.float32)
    tables_all = jnp.round(lax.all_gather(tables, axes, axis=0, tiled=True))
    target_tile = aperture.reshape(item_count)
    onehot = (target_tile[:, None] == jnp.arange(device_count, dtype=jnp.int32)[None, :]).astype(
        jnp.int32
    )
    before = jnp.cumsum(onehot, axis=0) - onehot
    slot_index = jnp.sum(before * onehot, axis=1)
    target_slot = target_tile * capacity + slot_index
    item_cells = (
        landing.reshape(block_count, per_block, aperture_len)
        .transpose(0, 2, 1)
        .reshape(item_count, per_block)
    )
    cell_send = (
        jnp.zeros((device_count * capacity, per_block), jnp.int32).at[target_slot].set(item_cells)
    )
    cell_recv = lax.all_to_all(
        cell_send.reshape(device_count, capacity * per_block),
        axes,
        split_axis=0,
        concat_axis=0,
        tiled=True,
    )
    cell_recv = cell_recv.reshape(device_count * capacity * per_block)
    tile_rows = image.reshape(cell_count, depth_len)
    weight_matrix = weights.reshape(samples, depth_len)
    contract = (((1,), (1,)), ((), ()))
    tile_table = lax.dot_general(
        tile_rows, weight_matrix, contract, preferred_element_type=jnp.float32
    )
    predicted = jnp.take(tile_table.astype(jnp.bfloat16), cell_recv, axis=0)
    outgoing = predicted.reshape(device_count, capacity * per_block, samples)
    returned = traverse(outgoing).reshape(device_count * capacity, per_block, samples)
    own_preds = jnp.take(returned, target_slot, axis=0).reshape(
        block_count, aperture_len, per_block, samples
    )
    synthetic = jnp.sum(own_preds.astype(jnp.float32), axis=1).reshape(trace_count, samples)
    half = wavelet.shape[0] // 2
    modeled = banded(synthetic, band_block(wavelet[::-1], half))
    residual = modeled - observed.astype(jnp.float32)
    adjoint = banded(residual, band_block(wavelet, half)).astype(jnp.bfloat16)

    adjoint_all = lax.all_gather(adjoint, axes, axis=0, tiled=True)
    all_blocks = block_count * device_count
    aperture_all = tables_all[:, :aperture_len].astype(jnp.int32)
    landing_all = tables_all[:, aperture_len:].astype(jnp.int32).reshape(all_blocks * per_block, aperture_len)
    relevant = capacity * device_count
    hit = aperture_all == me
    has = jnp.any(hit, axis=1)
    entry = jnp.argmax(hit, axis=1).astype(jnp.int32)
    position = jnp.cumsum(has.astype(jnp.int32)) - 1
    slot = jnp.where(has, position, relevant)
    chosen = (
        jnp.zeros((relevant,), jnp.int32)
        .at[slot]
        .set(jnp.arange(all_blocks, dtype=jnp.int32), mode="drop")
    )
    found = jnp.sum(has.astype(jnp.int32))
    cells_all = jnp.take_along_axis(
        landing_all.reshape(all_blocks, per_block, aperture_len), entry[:, None, None], axis=2
    )[:, :, 0]
    cells = jnp.where(
        (jnp.arange(relevant) < found)[:, None], jnp.take(cells_all, chosen, axis=0), cell_count
    )
    picked = jnp.take(adjoint_all.reshape(all_blocks, per_block, samples), chosen, axis=0)
    per_trace = jnp.dot(
        picked.reshape(relevant * per_block, samples),
        weight_matrix,
        preferred_element_type=jnp.float32,
    )
    raw_gradient = (
        jnp.zeros((cell_count, depth_len), jnp.float32)
        .at[cells.reshape(relevant * per_block)]
        .add(per_trace, mode="drop")
    )
    raw_gradient = raw_gradient.reshape(rows_x, rows_y, depth_len)
    raw_low, raw_high = halos(raw_gradient, "inline", 0, HW)
    smooth_x = smooth_zx(raw_gradient, raw_low, raw_high, taps)
    x_low, x_high = halos(smooth_x, "xline", 1, HW)
    gradient = smooth_y(smooth_x, x_low, x_high, taps)
    return (gradient, residual)


def solution(mesh):
    return jax.shard_map(
        local,
        mesh=mesh,
        in_specs=(
            P("inline", "xline", None),
            P("inline", "xline", None, None),
            P(("inline", "xline"), None),
            P(),
            P(),
            P(("inline", "xline"), None),
            P(("inline", "xline"), None),
        ),
        out_specs=(P("inline", "xline", None), P(("inline", "xline"), None)),
        check_vma=False,
    )
```

```python
import jax
import jax.numpy as jnp
from jax import lax
from jax.experimental import pallas as pl
from jax.experimental.pallas import tpu as pltpu
from jax.sharding import PartitionSpec as P

HW = 4


def _zx_kernel(taps_ref, main_ref, low_ref, high_ref, out_ref, ext_ref):
    nx = main_ref.shape[0]
    ext_ref[0:HW] = low_ref[...]
    ext_ref[HW:HW + nx] = main_ref[...]
    ext_ref[HW + nx:] = high_ref[...]
    depth = ext_ref.shape[2]
    x = ext_ref[...]
    lane = lax.broadcasted_iota(jnp.int32, x.shape, 2)
    acc = taps_ref[HW] * x
    for j in range(2 * HW + 1):
        if j == HW:
            continue
        shifted = pltpu.roll(x, (HW - j) % depth, 2)
        source = lane + (j - HW)
        keep = (source >= 0) & (source < depth)
        acc = acc + taps_ref[j] * jnp.where(keep, shifted, 0.0)
    ext_ref[...] = acc
    out = taps_ref[0] * ext_ref[0:nx]
    for j in range(1, 2 * HW + 1):
        out = out + taps_ref[j] * ext_ref[j:j + nx]
    out_ref[...] = out


def smooth_zx(raw, low, high, taps, blocks, ty=8):
    nx, ny, nz = raw.shape
    return pl.pallas_call(
        _zx_kernel,
        grid=(len(blocks),),
        in_specs=[
            pl.BlockSpec(memory_space=pltpu.SMEM),
            pl.BlockSpec((nx, ty, nz), lambda i: (0, blocks[0] + i * (blocks[-1] - blocks[0]) // max(1, len(blocks) - 1), 0)),
            pl.BlockSpec((HW, ty, nz), lambda i: (0, blocks[0] + i * (blocks[-1] - blocks[0]) // max(1, len(blocks) - 1), 0)),
            pl.BlockSpec((HW, ty, nz), lambda i: (0, blocks[0] + i * (blocks[-1] - blocks[0]) // max(1, len(blocks) - 1), 0)),
        ],
        out_specs=pl.BlockSpec((nx, ty, nz), lambda i: (0, i, 0)),
        out_shape=jax.ShapeDtypeStruct((nx, ty * len(blocks), nz), jnp.float32),
        scratch_shapes=[pltpu.VMEM((nx + 2 * HW, ty, nz), jnp.float32)],
        cost_estimate=pl.CostEstimate(
            flops=40 * nx * ty * nz * len(blocks), transcendentals=0,
            bytes_accessed=int(nx * ty * nz * len(blocks) * 10),
        ),
    )(taps, raw, low, high)


def _y_kernel(taps_ref, first_ref, middle_ref, last_ref, low_ref, high_ref, out_ref, ext_ref):
    edge = first_ref.shape[1]
    ny = middle_ref.shape[1] + 2 * edge
    ext_ref[:, HW:2 * HW] = low_ref[...]
    ext_ref[:, 2 * HW:2 * HW + edge] = first_ref[...]
    ext_ref[:, 2 * HW + edge:2 * HW + ny - edge] = middle_ref[...]
    ext_ref[:, 2 * HW + ny - edge:2 * HW + ny] = last_ref[...]
    ext_ref[:, 2 * HW + ny:3 * HW + ny] = high_ref[...]
    out = taps_ref[0] * ext_ref[:, pl.ds(HW, ny)]
    for j in range(1, 2 * HW + 1):
        out = out + taps_ref[j] * ext_ref[:, pl.ds(HW + j, ny)]
    out_ref[...] = out


def smooth_y(edges, middle, low, high, taps, tx=4):
    nx, two_edge, nz = edges.shape
    edge = two_edge // 2
    ny = middle.shape[1] + two_edge
    return pl.pallas_call(
        _y_kernel,
        grid=(nx // tx,),
        in_specs=[
            pl.BlockSpec(memory_space=pltpu.SMEM),
            pl.BlockSpec((tx, edge, nz), lambda i: (i, 0, 0)),
            pl.BlockSpec((tx, ny - 2 * edge, nz), lambda i: (i, 0, 0)),
            pl.BlockSpec((tx, edge, nz), lambda i: (i, 1, 0)),
            pl.BlockSpec((tx, HW, nz), lambda i: (i, 0, 0)),
            pl.BlockSpec((tx, HW, nz), lambda i: (i, 0, 0)),
        ],
        out_specs=pl.BlockSpec((tx, ny, nz), lambda i: (i, 0, 0)),
        out_shape=jax.ShapeDtypeStruct((nx, ny, nz), jnp.float32),
        scratch_shapes=[pltpu.VMEM((tx, ny + 4 * HW, nz), jnp.float32)],
        cost_estimate=pl.CostEstimate(
            flops=18 * nx * ny * nz, transcendentals=0, bytes_accessed=int(nx * ny * nz * 8.8)
        ),
    )(taps, edges, middle, edges, low, high)


CHUNK = 128
HALO = 64


def halos(block, axis, dim, width):
    count = lax.axis_size(axis)
    forward = [(i, i + 1) for i in range(count - 1)]
    backward = [(target, source) for source, target in forward]
    low = lax.ppermute(
        lax.slice_in_dim(block, block.shape[dim] - width, None, axis=dim), axis, forward
    )
    high = lax.ppermute(lax.slice_in_dim(block, 0, width, axis=dim), axis, backward)
    return low, high


def extended(block, sides, width):
    for axis, dim in sides:
        count = lax.axis_size(axis)
        forward = [(i, i + 1) for i in range(count - 1)]
        backward = [(target, source) for source, target in forward]
        low = lax.ppermute(
            lax.slice_in_dim(block, block.shape[dim] - width, None, axis=dim), axis, forward
        )
        high = lax.ppermute(lax.slice_in_dim(block, 0, width, axis=dim), axis, backward)
        block = jnp.concatenate([low, block, high], axis=dim)
    return block


def band_block(values, centre):
    k = jnp.arange(CHUNK + 2 * HALO)[:, None]
    n = jnp.arange(CHUNK)[None, :]
    tap = k - n - HALO + centre
    block = jnp.zeros((CHUNK + 2 * HALO, CHUNK), jnp.float32)
    for j in range(values.shape[0]):
        block = jnp.where(tap == j, values[j], block)
    return block


def split(x):
    high = lax.reduce_precision(x, exponent_bits=8, mantissa_bits=7)
    return high.astype(jnp.bfloat16), (x - high).astype(jnp.bfloat16)


def windows(x):
    rows, length = x.shape
    chunks = length // CHUNK
    padded = jnp.pad(x, ((0, 0), (HALO, HALO)))
    pieces = padded.reshape(rows, chunks + 1, CHUNK)
    joined = jnp.concatenate([pieces[:, :chunks], pieces[:, 1:]], axis=-1)
    return joined.reshape(rows * chunks, CHUNK + 2 * HALO)


def banded(signal, block):
    rows, length = signal.shape
    x_high, x_low = split(signal)
    b_high, b_low = lax.optimization_barrier(split(block))
    w_high, w_low = windows(x_high), windows(x_low)
    out = (
        jnp.dot(w_high, b_high, preferred_element_type=jnp.float32)
        + jnp.dot(w_high, b_low, preferred_element_type=jnp.float32)
        + jnp.dot(w_low, b_high, preferred_element_type=jnp.float32)
    )
    return out.reshape(rows, length)


def filter_padded(padded, taps, axis):
    length = padded.shape[axis] - 8
    shape_out = list(padded.shape)
    shape_out[axis] = length
    result = jnp.zeros(tuple(shape_out), jnp.float32)
    for offset in range(9):
        result = result + taps[offset] * lax.slice_in_dim(
            padded, offset, offset + length, axis=axis
        )
    return result


def traverse(blocks):
    return lax.all_to_all(blocks, ("inline", "xline"), split_axis=0, concat_axis=0, tiled=True)


def local(image, weights, observed, wavelet, taps, aperture, landing):
    axes = ("inline", "xline")
    device_count = lax.axis_size("inline") * lax.axis_size("xline")
    me = lax.axis_index("inline") * lax.axis_size("xline") + lax.axis_index("xline")
    block_count, aperture_len = aperture.shape
    trace_count, samples = observed.shape
    per_block = trace_count // block_count
    rows_x, rows_y, depth_len = image.shape
    cell_count = rows_x * rows_y
    capacity = 2 * max(1, block_count * aperture_len // device_count)
    item_count = block_count * aperture_len
    tables = jnp.concatenate(
        [aperture, landing.reshape(block_count, per_block * aperture_len)], axis=1
    ).astype(jnp.float32)
    tables_all = jnp.round(lax.all_gather(tables, axes, axis=0, tiled=True))
    target_tile = aperture.reshape(item_count)
    onehot = (target_tile[:, None] == jnp.arange(device_count, dtype=jnp.int32)[None, :]).astype(
        jnp.int32
    )
    before = jnp.cumsum(onehot, axis=0) - onehot
    slot_index = jnp.sum(before * onehot, axis=1)
    target_slot = target_tile * capacity + slot_index
    item_cells = (
        landing.reshape(block_count, per_block, aperture_len)
        .transpose(0, 2, 1)
        .reshape(item_count, per_block)
    )
    cell_send = (
        jnp.zeros((device_count * capacity, per_block), jnp.int32).at[target_slot].set(item_cells)
    )
    cell_recv = lax.all_to_all(
        cell_send.reshape(device_count, capacity * per_block),
        axes,
        split_axis=0,
        concat_axis=0,
        tiled=True,
    )
    cell_recv = cell_recv.reshape(device_count * capacity * per_block)
    tile_rows = image.reshape(cell_count, depth_len)
    weight_matrix = weights.reshape(samples, depth_len)
    contract = (((1,), (1,)), ((), ()))
    tile_table = lax.dot_general(
        tile_rows, weight_matrix, contract, preferred_element_type=jnp.float32
    )
    predicted = jnp.take(tile_table.astype(jnp.bfloat16), cell_recv, axis=0)
    outgoing = predicted.reshape(device_count, capacity * per_block, samples)
    returned = traverse(outgoing).reshape(device_count * capacity, per_block, samples)
    own_preds = jnp.take(returned, target_slot, axis=0).reshape(
        block_count, aperture_len, per_block, samples
    )
    synthetic = jnp.sum(own_preds.astype(jnp.float32), axis=1).reshape(trace_count, samples)
    half = wavelet.shape[0] // 2
    modeled = banded(synthetic, band_block(wavelet[::-1], half))
    residual = modeled - observed.astype(jnp.float32)
    adjoint = banded(residual, band_block(wavelet, half)).astype(jnp.bfloat16)

    adjoint_all = lax.all_gather(adjoint, axes, axis=0, tiled=True)
    all_blocks = block_count * device_count
    aperture_all = tables_all[:, :aperture_len].astype(jnp.int32)
    landing_all = tables_all[:, aperture_len:].astype(jnp.int32).reshape(all_blocks * per_block, aperture_len)
    relevant = capacity * device_count
    hit = aperture_all == me
    has = jnp.any(hit, axis=1)
    entry = jnp.argmax(hit, axis=1).astype(jnp.int32)
    position = jnp.cumsum(has.astype(jnp.int32)) - 1
    slot = jnp.where(has, position, relevant)
    chosen = (
        jnp.zeros((relevant,), jnp.int32)
        .at[slot]
        .set(jnp.arange(all_blocks, dtype=jnp.int32), mode="drop")
    )
    found = jnp.sum(has.astype(jnp.int32))
    cells_all = jnp.take_along_axis(
        landing_all.reshape(all_blocks, per_block, aperture_len), entry[:, None, None], axis=2
    )[:, :, 0]
    cells = jnp.where(
        (jnp.arange(relevant) < found)[:, None], jnp.take(cells_all, chosen, axis=0), cell_count
    )
    picked = jnp.take(adjoint_all.reshape(all_blocks, per_block, samples), chosen, axis=0)
    per_trace = jnp.dot(
        picked.reshape(relevant * per_block, samples),
        weight_matrix,
        preferred_element_type=jnp.float32,
    )
    raw_gradient = (
        jnp.zeros((cell_count, depth_len), jnp.float32)
        .at[cells.reshape(relevant * per_block)]
        .add(per_trace, mode="drop")
    )
    raw_gradient = raw_gradient.reshape(rows_x, rows_y, depth_len)
    raw_low, raw_high = halos(raw_gradient, "inline", 0, HW)
    y_blocks = rows_y // 8
    edges = smooth_zx(raw_gradient, raw_low, raw_high, taps, (0, y_blocks - 1))
    x_low, x_high = halos(edges, "xline", 1, HW)
    middle = smooth_zx(raw_gradient, raw_low, raw_high, taps, tuple(range(1, y_blocks - 1)))
    gradient = smooth_y(edges, middle, x_low, x_high, taps)
    return (gradient, residual)


def solution(mesh):
    return jax.shard_map(
        local,
        mesh=mesh,
        in_specs=(
            P("inline", "xline", None),
            P("inline", "xline", None, None),
            P(("inline", "xline"), None),
            P(),
            P(),
            P(("inline", "xline"), None),
            P(("inline", "xline"), None),
        ),
        out_specs=(P("inline", "xline", None), P(("inline", "xline"), None)),
        check_vma=False,
    )
```

```python
import jax
import jax.numpy as jnp
from jax import lax
from jax.experimental import pallas as pl
from jax.experimental.pallas import tpu as pltpu
from jax.sharding import PartitionSpec as P

HW = 4


def _zx_kernel(taps_ref, main_ref, low_ref, high_ref, out_ref, ext_ref):
    nx = main_ref.shape[0]
    ext_ref[0:HW] = low_ref[...]
    ext_ref[HW:HW + nx] = main_ref[...]
    ext_ref[HW + nx:] = high_ref[...]
    depth = ext_ref.shape[2]
    x = ext_ref[...]
    lane = lax.broadcasted_iota(jnp.int32, x.shape, 2)
    acc = taps_ref[HW] * x
    for j in range(2 * HW + 1):
        if j == HW:
            continue
        shifted = pltpu.roll(x, (HW - j) % depth, 2)
        source = lane + (j - HW)
        keep = (source >= 0) & (source < depth)
        acc = acc + taps_ref[j] * jnp.where(keep, shifted, 0.0)
    ext_ref[...] = acc
    out = taps_ref[0] * ext_ref[0:nx]
    for j in range(1, 2 * HW + 1):
        out = out + taps_ref[j] * ext_ref[j:j + nx]
    out_ref[...] = out


def smooth_zx(raw, low, high, taps, blocks, ty=8):
    nx, ny, nz = raw.shape
    return pl.pallas_call(
        _zx_kernel,
        grid=(len(blocks),),
        in_specs=[
            pl.BlockSpec(memory_space=pltpu.SMEM),
            pl.BlockSpec((nx, ty, nz), lambda i: (0, blocks[0] + i * (blocks[-1] - blocks[0]) // max(1, len(blocks) - 1), 0)),
            pl.BlockSpec((HW, ty, nz), lambda i: (0, blocks[0] + i * (blocks[-1] - blocks[0]) // max(1, len(blocks) - 1), 0)),
            pl.BlockSpec((HW, ty, nz), lambda i: (0, blocks[0] + i * (blocks[-1] - blocks[0]) // max(1, len(blocks) - 1), 0)),
        ],
        out_specs=pl.BlockSpec((nx, ty, nz), lambda i: (0, i, 0)),
        out_shape=jax.ShapeDtypeStruct((nx, ty * len(blocks), nz), jnp.float32),
        scratch_shapes=[pltpu.VMEM((nx + 2 * HW, ty, nz), jnp.float32)],
        cost_estimate=pl.CostEstimate(
            flops=40 * nx * ty * nz * len(blocks), transcendentals=0,
            bytes_accessed=int(nx * ty * nz * len(blocks) * 10),
        ),
    )(taps, raw, low, high)


def _y_kernel(taps_ref, first_ref, middle_ref, last_ref, low_ref, high_ref, out_ref, ext_ref):
    edge = first_ref.shape[1]
    ny = middle_ref.shape[1] + 2 * edge
    ext_ref[:, HW:2 * HW] = low_ref[...]
    ext_ref[:, 2 * HW:2 * HW + edge] = first_ref[...]
    ext_ref[:, 2 * HW + edge:2 * HW + ny - edge] = middle_ref[...]
    ext_ref[:, 2 * HW + ny - edge:2 * HW + ny] = last_ref[...]
    ext_ref[:, 2 * HW + ny:3 * HW + ny] = high_ref[...]
    out = taps_ref[0] * ext_ref[:, pl.ds(HW, ny)]
    for j in range(1, 2 * HW + 1):
        out = out + taps_ref[j] * ext_ref[:, pl.ds(HW + j, ny)]
    out_ref[...] = out


def smooth_y(edges, middle, low, high, taps, tx=4):
    nx, two_edge, nz = edges.shape
    edge = two_edge // 2
    ny = middle.shape[1] + two_edge
    return pl.pallas_call(
        _y_kernel,
        grid=(nx // tx,),
        in_specs=[
            pl.BlockSpec(memory_space=pltpu.SMEM),
            pl.BlockSpec((tx, edge, nz), lambda i: (i, 0, 0)),
            pl.BlockSpec((tx, ny - 2 * edge, nz), lambda i: (i, 0, 0)),
            pl.BlockSpec((tx, edge, nz), lambda i: (i, 1, 0)),
            pl.BlockSpec((tx, HW, nz), lambda i: (i, 0, 0)),
            pl.BlockSpec((tx, HW, nz), lambda i: (i, 0, 0)),
        ],
        out_specs=pl.BlockSpec((tx, ny, nz), lambda i: (i, 0, 0)),
        out_shape=jax.ShapeDtypeStruct((nx, ny, nz), jnp.float32),
        scratch_shapes=[pltpu.VMEM((tx, ny + 4 * HW, nz), jnp.float32)],
        cost_estimate=pl.CostEstimate(
            flops=18 * nx * ny * nz, transcendentals=0, bytes_accessed=int(nx * ny * nz * 8.8)
        ),
    )(taps, edges, middle, edges, low, high)


CHUNK = 128
HALO = 64


def halos(block, axis, dim, width):
    count = lax.axis_size(axis)
    forward = [(i, i + 1) for i in range(count - 1)]
    backward = [(target, source) for source, target in forward]
    low = lax.ppermute(
        lax.slice_in_dim(block, block.shape[dim] - width, None, axis=dim), axis, forward
    )
    high = lax.ppermute(lax.slice_in_dim(block, 0, width, axis=dim), axis, backward)
    return low, high


def extended(block, sides, width):
    for axis, dim in sides:
        count = lax.axis_size(axis)
        forward = [(i, i + 1) for i in range(count - 1)]
        backward = [(target, source) for source, target in forward]
        low = lax.ppermute(
            lax.slice_in_dim(block, block.shape[dim] - width, None, axis=dim), axis, forward
        )
        high = lax.ppermute(lax.slice_in_dim(block, 0, width, axis=dim), axis, backward)
        block = jnp.concatenate([low, block, high], axis=dim)
    return block


def band_block(values, centre):
    k = jnp.arange(CHUNK + 2 * HALO)[:, None]
    n = jnp.arange(CHUNK)[None, :]
    tap = k - n - HALO + centre
    block = jnp.zeros((CHUNK + 2 * HALO, CHUNK), jnp.float32)
    for j in range(values.shape[0]):
        block = jnp.where(tap == j, values[j], block)
    return block


def split(x):
    high = lax.reduce_precision(x, exponent_bits=8, mantissa_bits=7)
    return high.astype(jnp.bfloat16), (x - high).astype(jnp.bfloat16)


def windows(x):
    rows, length = x.shape
    chunks = length // CHUNK
    padded = jnp.pad(x, ((0, 0), (HALO, HALO)))
    pieces = padded.reshape(rows, chunks + 1, CHUNK)
    joined = jnp.concatenate([pieces[:, :chunks], pieces[:, 1:]], axis=-1)
    return joined.reshape(rows * chunks, CHUNK + 2 * HALO)


def banded(signal, block):
    rows, length = signal.shape
    x_high, x_low = split(signal)
    b_high, b_low = lax.optimization_barrier(split(block))
    w_high, w_low = windows(x_high), windows(x_low)
    out = (
        jnp.dot(w_high, b_high, preferred_element_type=jnp.float32)
        + jnp.dot(w_high, b_low, preferred_element_type=jnp.float32)
        + jnp.dot(w_low, b_high, preferred_element_type=jnp.float32)
    )
    return out.reshape(rows, length)


def filter_padded(padded, taps, axis):
    length = padded.shape[axis] - 8
    shape_out = list(padded.shape)
    shape_out[axis] = length
    result = jnp.zeros(tuple(shape_out), jnp.float32)
    for offset in range(9):
        result = result + taps[offset] * lax.slice_in_dim(
            padded, offset, offset + length, axis=axis
        )
    return result


def traverse(blocks):
    return lax.all_to_all(blocks, ("inline", "xline"), split_axis=0, concat_axis=0, tiled=True)


def local(image, weights, observed, wavelet, taps, aperture, landing):
    axes = ("inline", "xline")
    device_count = lax.axis_size("inline") * lax.axis_size("xline")
    me = lax.axis_index("inline") * lax.axis_size("xline") + lax.axis_index("xline")
    block_count, aperture_len = aperture.shape
    trace_count, samples = observed.shape
    per_block = trace_count // block_count
    rows_x, rows_y, depth_len = image.shape
    cell_count = rows_x * rows_y
    capacity = 2 * max(1, block_count * aperture_len // device_count)
    item_count = block_count * aperture_len
    target_tile = aperture.reshape(item_count)
    onehot = (target_tile[:, None] == jnp.arange(device_count, dtype=jnp.int32)[None, :]).astype(
        jnp.int32
    )
    before = jnp.cumsum(onehot, axis=0) - onehot
    slot_index = jnp.sum(before * onehot, axis=1)
    target_slot = target_tile * capacity + slot_index
    item_cells = (
        landing.reshape(block_count, per_block, aperture_len)
        .transpose(0, 2, 1)
        .reshape(item_count, per_block)
    )
    cell_send = (
        jnp.zeros((device_count * capacity, per_block), jnp.int32).at[target_slot].set(item_cells)
    )
    cell_recv = lax.all_to_all(
        cell_send.reshape(device_count, capacity * per_block),
        axes,
        split_axis=0,
        concat_axis=0,
        tiled=True,
    )
    cell_recv = cell_recv.reshape(device_count * capacity * per_block)
    tile_rows = image.reshape(cell_count, depth_len)
    weight_matrix = weights.reshape(samples, depth_len)
    contract = (((1,), (1,)), ((), ()))
    tile_table = lax.dot_general(
        tile_rows, weight_matrix, contract, preferred_element_type=jnp.float32
    )
    predicted = jnp.take(tile_table.astype(jnp.bfloat16), cell_recv, axis=0)
    outgoing = predicted.reshape(device_count, capacity * per_block, samples)
    returned = traverse(outgoing).reshape(device_count * capacity, per_block, samples)
    own_preds = jnp.take(returned, target_slot, axis=0).reshape(
        block_count, aperture_len, per_block, samples
    )
    synthetic = jnp.sum(own_preds.astype(jnp.float32), axis=1).reshape(trace_count, samples)
    half = wavelet.shape[0] // 2
    modeled = banded(synthetic, band_block(wavelet[::-1], half))
    residual = modeled - observed.astype(jnp.float32)
    adjoint = banded(residual, band_block(wavelet, half)).astype(jnp.bfloat16)

    extra = 128
    coded = jnp.concatenate(
        [
            jnp.repeat(aperture, per_block, axis=0),
            landing // 64,
            landing % 64,
            jnp.zeros((trace_count, extra - 3 * aperture_len), jnp.int32),
        ],
        axis=1,
    ).astype(jnp.bfloat16)
    half_s = samples // 2
    first_all = lax.all_gather(
        jnp.concatenate([adjoint[:, :half_s], coded], axis=1), axes, axis=0, tiled=True
    )
    second_all = lax.all_gather(adjoint[:, half_s:], axes, axis=0, tiled=True)
    all_blocks = block_count * device_count
    codes = first_all[:, half_s:half_s + 3 * aperture_len].astype(jnp.int32)
    aperture_all = codes.reshape(all_blocks, per_block, 3 * aperture_len)[:, 0, :aperture_len]
    landing_all = (
        codes[:, aperture_len:2 * aperture_len] * 64 + codes[:, 2 * aperture_len:3 * aperture_len]
    )
    relevant = capacity * device_count
    hit = aperture_all == me
    has = jnp.any(hit, axis=1)
    entry = jnp.argmax(hit, axis=1).astype(jnp.int32)
    position = jnp.cumsum(has.astype(jnp.int32)) - 1
    slot = jnp.where(has, position, relevant)
    chosen = (
        jnp.zeros((relevant,), jnp.int32)
        .at[slot]
        .set(jnp.arange(all_blocks, dtype=jnp.int32), mode="drop")
    )
    found = jnp.sum(has.astype(jnp.int32))
    cells_all = jnp.take_along_axis(
        landing_all.reshape(all_blocks, per_block, aperture_len), entry[:, None, None], axis=2
    )[:, :, 0]
    cells = jnp.where(
        (jnp.arange(relevant) < found)[:, None], jnp.take(cells_all, chosen, axis=0), cell_count
    )
    picked_first = jnp.take(
        first_all[:, :half_s].reshape(all_blocks, per_block, half_s), chosen, axis=0
    )
    per_trace = jnp.dot(
        picked_first.reshape(relevant * per_block, half_s),
        weight_matrix[:half_s],
        preferred_element_type=jnp.float32,
    )
    picked_second = jnp.take(second_all.reshape(all_blocks, per_block, half_s), chosen, axis=0)
    per_trace = per_trace + jnp.dot(
        picked_second.reshape(relevant * per_block, half_s),
        weight_matrix[half_s:],
        preferred_element_type=jnp.float32,
    )
    raw_gradient = (
        jnp.zeros((cell_count, depth_len), jnp.float32)
        .at[cells.reshape(relevant * per_block)]
        .add(per_trace, mode="drop")
    )
    raw_gradient = raw_gradient.reshape(rows_x, rows_y, depth_len)
    raw_low, raw_high = halos(raw_gradient, "inline", 0, HW)
    y_blocks = rows_y // 8
    edges = smooth_zx(raw_gradient, raw_low, raw_high, taps, (0, y_blocks - 1))
    x_low, x_high = halos(edges, "xline", 1, HW)
    middle = smooth_zx(raw_gradient, raw_low, raw_high, taps, tuple(range(1, y_blocks - 1)))
    gradient = smooth_y(edges, middle, x_low, x_high, taps)
    return (gradient, residual)


def solution(mesh):
    return jax.shard_map(
        local,
        mesh=mesh,
        in_specs=(
            P("inline", "xline", None),
            P("inline", "xline", None, None),
            P(("inline", "xline"), None),
            P(),
            P(),
            P(("inline", "xline"), None),
            P(("inline", "xline"), None),
        ),
        out_specs=(P("inline", "xline", None), P(("inline", "xline"), None)),
        check_vma=False,
    )
```

```python
import jax
import jax.numpy as jnp
from jax import lax
from jax.experimental import pallas as pl
from jax.experimental.pallas import tpu as pltpu
from jax.sharding import PartitionSpec as P

HW = 4


def _zx_kernel(taps_ref, main_ref, low_ref, high_ref, out_ref, ext_ref):
    nx = main_ref.shape[0]
    ext_ref[0:HW] = low_ref[...]
    ext_ref[HW:HW + nx] = main_ref[...]
    ext_ref[HW + nx:] = high_ref[...]
    depth = ext_ref.shape[2]
    x = ext_ref[...]
    lane = lax.broadcasted_iota(jnp.int32, x.shape, 2)
    acc = taps_ref[HW] * x
    for j in range(2 * HW + 1):
        if j == HW:
            continue
        shifted = pltpu.roll(x, (HW - j) % depth, 2)
        source = lane + (j - HW)
        keep = (source >= 0) & (source < depth)
        acc = acc + taps_ref[j] * jnp.where(keep, shifted, 0.0)
    ext_ref[...] = acc
    out = taps_ref[0] * ext_ref[0:nx]
    for j in range(1, 2 * HW + 1):
        out = out + taps_ref[j] * ext_ref[j:j + nx]
    out_ref[...] = out


def smooth_zx(raw, low, high, taps, blocks, ty=8):
    nx, ny, nz = raw.shape
    return pl.pallas_call(
        _zx_kernel,
        grid=(len(blocks),),
        in_specs=[
            pl.BlockSpec(memory_space=pltpu.SMEM),
            pl.BlockSpec((nx, ty, nz), lambda i: (0, blocks[0] + i * (blocks[-1] - blocks[0]) // max(1, len(blocks) - 1), 0)),
            pl.BlockSpec((HW, ty, nz), lambda i: (0, blocks[0] + i * (blocks[-1] - blocks[0]) // max(1, len(blocks) - 1), 0)),
            pl.BlockSpec((HW, ty, nz), lambda i: (0, blocks[0] + i * (blocks[-1] - blocks[0]) // max(1, len(blocks) - 1), 0)),
        ],
        out_specs=pl.BlockSpec((nx, ty, nz), lambda i: (0, i, 0)),
        out_shape=jax.ShapeDtypeStruct((nx, ty * len(blocks), nz), jnp.float32),
        scratch_shapes=[pltpu.VMEM((nx + 2 * HW, ty, nz), jnp.float32)],
        cost_estimate=pl.CostEstimate(
            flops=40 * nx * ty * nz * len(blocks), transcendentals=0,
            bytes_accessed=int(nx * ty * nz * len(blocks) * 10),
        ),
    )(taps, raw, low, high)


def _y_kernel(taps_ref, first_ref, middle_ref, last_ref, low_ref, high_ref, out_ref, ext_ref):
    edge = first_ref.shape[1]
    ny = middle_ref.shape[1] + 2 * edge
    ext_ref[:, HW:2 * HW] = low_ref[...]
    ext_ref[:, 2 * HW:2 * HW + edge] = first_ref[...]
    ext_ref[:, 2 * HW + edge:2 * HW + ny - edge] = middle_ref[...]
    ext_ref[:, 2 * HW + ny - edge:2 * HW + ny] = last_ref[...]
    ext_ref[:, 2 * HW + ny:3 * HW + ny] = high_ref[...]
    out = taps_ref[0] * ext_ref[:, pl.ds(HW, ny)]
    for j in range(1, 2 * HW + 1):
        out = out + taps_ref[j] * ext_ref[:, pl.ds(HW + j, ny)]
    out_ref[...] = out


def smooth_y(edges, middle, low, high, taps, tx=4):
    nx, two_edge, nz = edges.shape
    edge = two_edge // 2
    ny = middle.shape[1] + two_edge
    return pl.pallas_call(
        _y_kernel,
        grid=(nx // tx,),
        in_specs=[
            pl.BlockSpec(memory_space=pltpu.SMEM),
            pl.BlockSpec((tx, edge, nz), lambda i: (i, 0, 0)),
            pl.BlockSpec((tx, ny - 2 * edge, nz), lambda i: (i, 0, 0)),
            pl.BlockSpec((tx, edge, nz), lambda i: (i, 1, 0)),
            pl.BlockSpec((tx, HW, nz), lambda i: (i, 0, 0)),
            pl.BlockSpec((tx, HW, nz), lambda i: (i, 0, 0)),
        ],
        out_specs=pl.BlockSpec((tx, ny, nz), lambda i: (i, 0, 0)),
        out_shape=jax.ShapeDtypeStruct((nx, ny, nz), jnp.float32),
        scratch_shapes=[pltpu.VMEM((tx, ny + 4 * HW, nz), jnp.float32)],
        cost_estimate=pl.CostEstimate(
            flops=18 * nx * ny * nz, transcendentals=0, bytes_accessed=int(nx * ny * nz * 8.8)
        ),
    )(taps, edges, middle, edges, low, high)


CHUNK = 128
HALO = 64


def halos(block, axis, dim, width):
    count = lax.axis_size(axis)
    forward = [(i, i + 1) for i in range(count - 1)]
    backward = [(target, source) for source, target in forward]
    low = lax.ppermute(
        lax.slice_in_dim(block, block.shape[dim] - width, None, axis=dim), axis, forward
    )
    high = lax.ppermute(lax.slice_in_dim(block, 0, width, axis=dim), axis, backward)
    return low, high


def extended(block, sides, width):
    for axis, dim in sides:
        count = lax.axis_size(axis)
        forward = [(i, i + 1) for i in range(count - 1)]
        backward = [(target, source) for source, target in forward]
        low = lax.ppermute(
            lax.slice_in_dim(block, block.shape[dim] - width, None, axis=dim), axis, forward
        )
        high = lax.ppermute(lax.slice_in_dim(block, 0, width, axis=dim), axis, backward)
        block = jnp.concatenate([low, block, high], axis=dim)
    return block


def band_block(values, centre):
    k = jnp.arange(CHUNK + 2 * HALO)[:, None]
    n = jnp.arange(CHUNK)[None, :]
    tap = k - n - HALO + centre
    block = jnp.zeros((CHUNK + 2 * HALO, CHUNK), jnp.float32)
    for j in range(values.shape[0]):
        block = jnp.where(tap == j, values[j], block)
    return block


def split(x):
    high = lax.reduce_precision(x, exponent_bits=8, mantissa_bits=7)
    return high.astype(jnp.bfloat16), (x - high).astype(jnp.bfloat16)


def windows(x):
    rows, length = x.shape
    chunks = length // CHUNK
    padded = jnp.pad(x, ((0, 0), (HALO, HALO)))
    pieces = padded.reshape(rows, chunks + 1, CHUNK)
    joined = jnp.concatenate([pieces[:, :chunks], pieces[:, 1:]], axis=-1)
    return joined.reshape(rows * chunks, CHUNK + 2 * HALO)


def banded(signal, block):
    rows, length = signal.shape
    x_high, x_low = split(signal)
    b_high, b_low = lax.optimization_barrier(split(block))
    w_high, w_low = windows(x_high), windows(x_low)
    out = (
        jnp.dot(w_high, b_high, preferred_element_type=jnp.float32)
        + jnp.dot(w_high, b_low, preferred_element_type=jnp.float32)
        + jnp.dot(w_low, b_high, preferred_element_type=jnp.float32)
    )
    return out.reshape(rows, length)


def filter_padded(padded, taps, axis):
    length = padded.shape[axis] - 8
    shape_out = list(padded.shape)
    shape_out[axis] = length
    result = jnp.zeros(tuple(shape_out), jnp.float32)
    for offset in range(9):
        result = result + taps[offset] * lax.slice_in_dim(
            padded, offset, offset + length, axis=axis
        )
    return result


def traverse(blocks):
    return lax.all_to_all(blocks, ("inline", "xline"), split_axis=0, concat_axis=0, tiled=True)


def local(image, weights, observed, wavelet, taps, aperture, landing):
    axes = ("inline", "xline")
    device_count = lax.axis_size("inline") * lax.axis_size("xline")
    me = lax.axis_index("inline") * lax.axis_size("xline") + lax.axis_index("xline")
    block_count, aperture_len = aperture.shape
    trace_count, samples = observed.shape
    per_block = trace_count // block_count
    rows_x, rows_y, depth_len = image.shape
    cell_count = rows_x * rows_y
    capacity = 2 * max(1, block_count * aperture_len // device_count)
    item_count = block_count * aperture_len
    tables = jnp.concatenate(
        [aperture, landing.reshape(block_count, per_block * aperture_len)], axis=1
    ).astype(jnp.float32)
    tables_all = jnp.round(lax.all_gather(tables, axes, axis=0, tiled=True))
    target_tile = aperture.reshape(item_count)
    onehot = (target_tile[:, None] == jnp.arange(device_count, dtype=jnp.int32)[None, :]).astype(
        jnp.int32
    )
    before = jnp.cumsum(onehot, axis=0) - onehot
    slot_index = jnp.sum(before * onehot, axis=1)
    target_slot = target_tile * capacity + slot_index
    item_cells = (
        landing.reshape(block_count, per_block, aperture_len)
        .transpose(0, 2, 1)
        .reshape(item_count, per_block)
    )
    cell_send = (
        jnp.zeros((device_count * capacity, per_block), jnp.int32).at[target_slot].set(item_cells)
    )
    cell_recv = lax.all_to_all(
        cell_send.reshape(device_count, capacity * per_block),
        axes,
        split_axis=0,
        concat_axis=0,
        tiled=True,
    )
    cell_recv = cell_recv.reshape(device_count * capacity * per_block)
    tile_rows = image.reshape(cell_count, depth_len)
    weight_matrix = weights.reshape(samples, depth_len)
    contract = (((1,), (1,)), ((), ()))
    half_cap = capacity // 2
    requests = cell_recv.reshape(device_count, capacity, per_block)
    returned = []
    for part in range(2):
        wanted = requests[:, part * half_cap:(part + 1) * half_cap].reshape(-1)
        predicted = lax.dot_general(
            jnp.take(tile_rows, wanted, axis=0), weight_matrix, contract,
            preferred_element_type=jnp.float32,
        ).astype(jnp.bfloat16)
        returned.append(
            traverse(predicted.reshape(device_count, half_cap * per_block, samples)).reshape(
                device_count * half_cap, per_block, samples
            )
        )
    tile_of = target_tile
    within = slot_index % half_cap
    from_first = jnp.take(returned[0], tile_of * half_cap + within, axis=0)
    from_second = jnp.take(returned[1], tile_of * half_cap + within, axis=0)
    own_preds = jnp.where(
        (slot_index < half_cap)[:, None, None], from_first, from_second
    ).reshape(block_count, aperture_len, per_block, samples)
    synthetic = jnp.sum(own_preds.astype(jnp.float32), axis=1).reshape(trace_count, samples)
    half = wavelet.shape[0] // 2
    modeled = banded(synthetic, band_block(wavelet[::-1], half))
    residual = modeled - observed.astype(jnp.float32)
    adjoint = banded(residual, band_block(wavelet, half)).astype(jnp.bfloat16)

    adjoint_all = lax.all_gather(adjoint, axes, axis=0, tiled=True)
    all_blocks = block_count * device_count
    aperture_all = tables_all[:, :aperture_len].astype(jnp.int32)
    landing_all = tables_all[:, aperture_len:].astype(jnp.int32).reshape(all_blocks * per_block, aperture_len)
    relevant = capacity * device_count
    hit = aperture_all == me
    has = jnp.any(hit, axis=1)
    entry = jnp.argmax(hit, axis=1).astype(jnp.int32)
    position = jnp.cumsum(has.astype(jnp.int32)) - 1
    slot = jnp.where(has, position, relevant)
    chosen = (
        jnp.zeros((relevant,), jnp.int32)
        .at[slot]
        .set(jnp.arange(all_blocks, dtype=jnp.int32), mode="drop")
    )
    found = jnp.sum(has.astype(jnp.int32))
    cells_all = jnp.take_along_axis(
        landing_all.reshape(all_blocks, per_block, aperture_len), entry[:, None, None], axis=2
    )[:, :, 0]
    cells = jnp.where(
        (jnp.arange(relevant) < found)[:, None], jnp.take(cells_all, chosen, axis=0), cell_count
    )
    picked = jnp.take(adjoint_all.reshape(all_blocks, per_block, samples), chosen, axis=0)
    per_trace = jnp.dot(
        picked.reshape(relevant * per_block, samples),
        weight_matrix,
        preferred_element_type=jnp.float32,
    )
    raw_gradient = (
        jnp.zeros((cell_count, depth_len), jnp.float32)
        .at[cells.reshape(relevant * per_block)]
        .add(per_trace, mode="drop")
    )
    raw_gradient = raw_gradient.reshape(rows_x, rows_y, depth_len)
    raw_low, raw_high = halos(raw_gradient, "inline", 0, HW)
    y_blocks = rows_y // 8
    edges = smooth_zx(raw_gradient, raw_low, raw_high, taps, (0, y_blocks - 1))
    x_low, x_high = halos(edges, "xline", 1, HW)
    middle = smooth_zx(raw_gradient, raw_low, raw_high, taps, tuple(range(1, y_blocks - 1)))
    gradient = smooth_y(edges, middle, x_low, x_high, taps)
    return (gradient, residual)


def solution(mesh):
    return jax.shard_map(
        local,
        mesh=mesh,
        in_specs=(
            P("inline", "xline", None),
            P("inline", "xline", None, None),
            P(("inline", "xline"), None),
            P(),
            P(),
            P(("inline", "xline"), None),
            P(("inline", "xline"), None),
        ),
        out_specs=(P("inline", "xline", None), P(("inline", "xline"), None)),
        check_vma=False,
    )
```

```python
import jax
import jax.numpy as jnp
from jax import lax
from jax.experimental import pallas as pl
from jax.experimental.pallas import tpu as pltpu
from jax.sharding import PartitionSpec as P

HW = 4


def _zx_kernel(taps_ref, main_ref, low_ref, high_ref, out_ref, ext_ref):
    nx = main_ref.shape[0]
    depth = main_ref.shape[2]
    ext_ref[:, :, depth:] = jnp.zeros(ext_ref.shape[:2] + (ext_ref.shape[2] - depth,), jnp.float32)
    ext_ref[0:HW, :, :depth] = low_ref[...]
    ext_ref[HW:HW + nx, :, :depth] = main_ref[...]
    ext_ref[HW + nx:, :, :depth] = high_ref[...]
    x = ext_ref[...]
    wide = x.shape[2]
    acc = taps_ref[HW] * x
    for j in range(2 * HW + 1):
        if j == HW:
            continue
        acc = acc + taps_ref[j] * pltpu.roll(x, (HW - j) % wide, 2)
    ext_ref[...] = acc
    out = taps_ref[0] * ext_ref[0:nx, :, :depth]
    for j in range(1, 2 * HW + 1):
        out = out + taps_ref[j] * ext_ref[j:j + nx, :, :depth]
    out_ref[...] = out


def smooth_zx(raw, low, high, taps, blocks, ty=8):
    nx, ny, nz = raw.shape
    return pl.pallas_call(
        _zx_kernel,
        grid=(len(blocks),),
        in_specs=[
            pl.BlockSpec(memory_space=pltpu.SMEM),
            pl.BlockSpec((nx, ty, nz), lambda i: (0, blocks[0] + i * (blocks[-1] - blocks[0]) // max(1, len(blocks) - 1), 0)),
            pl.BlockSpec((HW, ty, nz), lambda i: (0, blocks[0] + i * (blocks[-1] - blocks[0]) // max(1, len(blocks) - 1), 0)),
            pl.BlockSpec((HW, ty, nz), lambda i: (0, blocks[0] + i * (blocks[-1] - blocks[0]) // max(1, len(blocks) - 1), 0)),
        ],
        out_specs=pl.BlockSpec((nx, ty, nz), lambda i: (0, i, 0)),
        out_shape=jax.ShapeDtypeStruct((nx, ty * len(blocks), nz), jnp.float32),
        scratch_shapes=[pltpu.VMEM((nx + 2 * HW, ty, nz + 128), jnp.float32)],
        cost_estimate=pl.CostEstimate(
            flops=40 * nx * ty * nz * len(blocks), transcendentals=0,
            bytes_accessed=int(nx * ty * nz * len(blocks) * 10),
        ),
    )(taps, raw, low, high)


def _y_kernel(taps_ref, first_ref, middle_ref, last_ref, low_ref, high_ref, out_ref, ext_ref):
    edge = first_ref.shape[1]
    ny = middle_ref.shape[1] + 2 * edge
    ext_ref[:, HW:2 * HW] = low_ref[...]
    ext_ref[:, 2 * HW:2 * HW + edge] = first_ref[...]
    ext_ref[:, 2 * HW + edge:2 * HW + ny - edge] = middle_ref[...]
    ext_ref[:, 2 * HW + ny - edge:2 * HW + ny] = last_ref[...]
    ext_ref[:, 2 * HW + ny:3 * HW + ny] = high_ref[...]
    out = taps_ref[0] * ext_ref[:, pl.ds(HW, ny)]
    for j in range(1, 2 * HW + 1):
        out = out + taps_ref[j] * ext_ref[:, pl.ds(HW + j, ny)]
    out_ref[...] = out


def smooth_y(edges, middle, low, high, taps, tx=4):
    nx, two_edge, nz = edges.shape
    edge = two_edge // 2
    ny = middle.shape[1] + two_edge
    return pl.pallas_call(
        _y_kernel,
        grid=(nx // tx,),
        in_specs=[
            pl.BlockSpec(memory_space=pltpu.SMEM),
            pl.BlockSpec((tx, edge, nz), lambda i: (i, 0, 0)),
            pl.BlockSpec((tx, ny - 2 * edge, nz), lambda i: (i, 0, 0)),
            pl.BlockSpec((tx, edge, nz), lambda i: (i, 1, 0)),
            pl.BlockSpec((tx, HW, nz), lambda i: (i, 0, 0)),
            pl.BlockSpec((tx, HW, nz), lambda i: (i, 0, 0)),
        ],
        out_specs=pl.BlockSpec((tx, ny, nz), lambda i: (i, 0, 0)),
        out_shape=jax.ShapeDtypeStruct((nx, ny, nz), jnp.float32),
        scratch_shapes=[pltpu.VMEM((tx, ny + 4 * HW, nz), jnp.float32)],
        cost_estimate=pl.CostEstimate(
            flops=18 * nx * ny * nz, transcendentals=0, bytes_accessed=int(nx * ny * nz * 8.8)
        ),
    )(taps, edges, middle, edges, low, high)


CHUNK = 128
HALO = 64


def halos(block, axis, dim, width):
    count = lax.axis_size(axis)
    forward = [(i, i + 1) for i in range(count - 1)]
    backward = [(target, source) for source, target in forward]
    low = lax.ppermute(
        lax.slice_in_dim(block, block.shape[dim] - width, None, axis=dim), axis, forward
    )
    high = lax.ppermute(lax.slice_in_dim(block, 0, width, axis=dim), axis, backward)
    return low, high


def extended(block, sides, width):
    for axis, dim in sides:
        count = lax.axis_size(axis)
        forward = [(i, i + 1) for i in range(count - 1)]
        backward = [(target, source) for source, target in forward]
        low = lax.ppermute(
            lax.slice_in_dim(block, block.shape[dim] - width, None, axis=dim), axis, forward
        )
        high = lax.ppermute(lax.slice_in_dim(block, 0, width, axis=dim), axis, backward)
        block = jnp.concatenate([low, block, high], axis=dim)
    return block


def band_block(values, centre):
    k = jnp.arange(CHUNK + 2 * HALO)[:, None]
    n = jnp.arange(CHUNK)[None, :]
    tap = k - n - HALO + centre
    block = jnp.zeros((CHUNK + 2 * HALO, CHUNK), jnp.float32)
    for j in range(values.shape[0]):
        block = jnp.where(tap == j, values[j], block)
    return block


def split(x):
    high = lax.reduce_precision(x, exponent_bits=8, mantissa_bits=7)
    return high.astype(jnp.bfloat16), (x - high).astype(jnp.bfloat16)


def windows(x):
    rows, length = x.shape
    chunks = length // CHUNK
    padded = jnp.pad(x, ((0, 0), (HALO, HALO)))
    pieces = padded.reshape(rows, chunks + 1, CHUNK)
    joined = jnp.concatenate([pieces[:, :chunks], pieces[:, 1:]], axis=-1)
    return joined.reshape(rows * chunks, CHUNK + 2 * HALO)


def banded(signal, block):
    rows, length = signal.shape
    x_high, x_low = split(signal)
    b_high, b_low = lax.optimization_barrier(split(block))
    w_high, w_low = windows(x_high), windows(x_low)
    out = (
        jnp.dot(w_high, b_high, preferred_element_type=jnp.float32)
        + jnp.dot(w_high, b_low, preferred_element_type=jnp.float32)
        + jnp.dot(w_low, b_high, preferred_element_type=jnp.float32)
    )
    return out.reshape(rows, length)


def filter_padded(padded, taps, axis):
    length = padded.shape[axis] - 8
    shape_out = list(padded.shape)
    shape_out[axis] = length
    result = jnp.zeros(tuple(shape_out), jnp.float32)
    for offset in range(9):
        result = result + taps[offset] * lax.slice_in_dim(
            padded, offset, offset + length, axis=axis
        )
    return result


def traverse(blocks):
    return lax.all_to_all(blocks, ("inline", "xline"), split_axis=0, concat_axis=0, tiled=True)


def local(image, weights, observed, wavelet, taps, aperture, landing):
    axes = ("inline", "xline")
    device_count = lax.axis_size("inline") * lax.axis_size("xline")
    me = lax.axis_index("inline") * lax.axis_size("xline") + lax.axis_index("xline")
    block_count, aperture_len = aperture.shape
    trace_count, samples = observed.shape
    per_block = trace_count // block_count
    rows_x, rows_y, depth_len = image.shape
    cell_count = rows_x * rows_y
    capacity = 2 * max(1, block_count * aperture_len // device_count)
    item_count = block_count * aperture_len
    tables = jnp.concatenate(
        [aperture, landing.reshape(block_count, per_block * aperture_len)], axis=1
    ).astype(jnp.float32)
    tables_all = jnp.round(lax.all_gather(tables, axes, axis=0, tiled=True))
    target_tile = aperture.reshape(item_count)
    onehot = (target_tile[:, None] == jnp.arange(device_count, dtype=jnp.int32)[None, :]).astype(
        jnp.int32
    )
    before = jnp.cumsum(onehot, axis=0) - onehot
    slot_index = jnp.sum(before * onehot, axis=1)
    target_slot = target_tile * capacity + slot_index
    item_cells = (
        landing.reshape(block_count, per_block, aperture_len)
        .transpose(0, 2, 1)
        .reshape(item_count, per_block)
    )
    cell_send = (
        jnp.zeros((device_count * capacity, per_block), jnp.int32).at[target_slot].set(item_cells)
    )
    cell_recv = lax.all_to_all(
        cell_send.reshape(device_count, capacity * per_block),
        axes,
        split_axis=0,
        concat_axis=0,
        tiled=True,
    )
    cell_recv = cell_recv.reshape(device_count * capacity * per_block)
    tile_rows = image.reshape(cell_count, depth_len)
    weight_matrix = weights.reshape(samples, depth_len)
    contract = (((1,), (1,)), ((), ()))
    half_cap = capacity // 2
    requests = cell_recv.reshape(device_count, capacity, per_block)
    returned = []
    for part in range(2):
        wanted = requests[:, part * half_cap:(part + 1) * half_cap].reshape(-1)
        predicted = lax.dot_general(
            jnp.take(tile_rows, wanted, axis=0), weight_matrix, contract,
            preferred_element_type=jnp.float32,
        ).astype(jnp.bfloat16)
        returned.append(
            traverse(predicted.reshape(device_count, half_cap * per_block, samples)).reshape(
                device_count * half_cap, per_block, samples
            )
        )
    tile_of = target_tile
    within = slot_index % half_cap
    from_first = jnp.take(returned[0], tile_of * half_cap + within, axis=0)
    from_second = jnp.take(returned[1], tile_of * half_cap + within, axis=0)
    own_preds = jnp.where(
        (slot_index < half_cap)[:, None, None], from_first, from_second
    ).reshape(block_count, aperture_len, per_block, samples)
    synthetic = jnp.sum(own_preds.astype(jnp.float32), axis=1).reshape(trace_count, samples)
    half = wavelet.shape[0] // 2
    modeled = banded(synthetic, band_block(wavelet[::-1], half))
    residual = modeled - observed.astype(jnp.float32)
    adjoint = banded(residual, band_block(wavelet, half)).astype(jnp.bfloat16)

    adjoint_all = lax.all_gather(adjoint, axes, axis=0, tiled=True)
    all_blocks = block_count * device_count
    aperture_all = tables_all[:, :aperture_len].astype(jnp.int32)
    landing_all = tables_all[:, aperture_len:].astype(jnp.int32).reshape(all_blocks * per_block, aperture_len)
    relevant = capacity * device_count
    hit = aperture_all == me
    has = jnp.any(hit, axis=1)
    entry = jnp.argmax(hit, axis=1).astype(jnp.int32)
    position = jnp.cumsum(has.astype(jnp.int32)) - 1
    slot = jnp.where(has, position, relevant)
    chosen = (
        jnp.zeros((relevant,), jnp.int32)
        .at[slot]
        .set(jnp.arange(all_blocks, dtype=jnp.int32), mode="drop")
    )
    found = jnp.sum(has.astype(jnp.int32))
    cells_all = jnp.take_along_axis(
        landing_all.reshape(all_blocks, per_block, aperture_len), entry[:, None, None], axis=2
    )[:, :, 0]
    cells = jnp.where(
        (jnp.arange(relevant) < found)[:, None], jnp.take(cells_all, chosen, axis=0), cell_count
    )
    picked = jnp.take(adjoint_all.reshape(all_blocks, per_block, samples), chosen, axis=0)
    per_trace = jnp.dot(
        picked.reshape(relevant * per_block, samples),
        weight_matrix,
        preferred_element_type=jnp.float32,
    )
    raw_gradient = (
        jnp.zeros((cell_count, depth_len), jnp.float32)
        .at[cells.reshape(relevant * per_block)]
        .add(per_trace, mode="drop")
    )
    raw_gradient = raw_gradient.reshape(rows_x, rows_y, depth_len)
    raw_low, raw_high = halos(raw_gradient, "inline", 0, HW)
    y_blocks = rows_y // 8
    edges = smooth_zx(raw_gradient, raw_low, raw_high, taps, (0, y_blocks - 1))
    x_low, x_high = halos(edges, "xline", 1, HW)
    middle = smooth_zx(raw_gradient, raw_low, raw_high, taps, tuple(range(1, y_blocks - 1)))
    gradient = smooth_y(edges, middle, x_low, x_high, taps)
    return (gradient, residual)


def solution(mesh):
    return jax.shard_map(
        local,
        mesh=mesh,
        in_specs=(
            P("inline", "xline", None),
            P("inline", "xline", None, None),
            P(("inline", "xline"), None),
            P(),
            P(),
            P(("inline", "xline"), None),
            P(("inline", "xline"), None),
        ),
        out_specs=(P("inline", "xline", None), P(("inline", "xline"), None)),
        check_vma=False,
    )
```

```python
import jax
import jax.numpy as jnp
from jax import lax
from jax.experimental import pallas as pl
from jax.experimental.pallas import tpu as pltpu
from jax.sharding import PartitionSpec as P

HW = 4


def _zx_kernel(taps_ref, main_ref, low_ref, high_ref, out_ref, ext_ref):
    nx = main_ref.shape[0]
    ext_ref[0:HW] = low_ref[...]
    ext_ref[HW:HW + nx] = main_ref[...]
    ext_ref[HW + nx:] = high_ref[...]
    out = taps_ref[0] * ext_ref[0:nx]
    for j in range(1, 2 * HW + 1):
        out = out + taps_ref[j] * ext_ref[j:j + nx]
    out_ref[...] = out


def smooth_zx(raw, low, high, taps, blocks, ty=8):
    nx, ny, nz = raw.shape
    return pl.pallas_call(
        _zx_kernel,
        grid=(len(blocks),),
        in_specs=[
            pl.BlockSpec(memory_space=pltpu.SMEM),
            pl.BlockSpec((nx, ty, nz), lambda i: (0, blocks[0] + i * (blocks[-1] - blocks[0]) // max(1, len(blocks) - 1), 0)),
            pl.BlockSpec((HW, ty, nz), lambda i: (0, blocks[0] + i * (blocks[-1] - blocks[0]) // max(1, len(blocks) - 1), 0)),
            pl.BlockSpec((HW, ty, nz), lambda i: (0, blocks[0] + i * (blocks[-1] - blocks[0]) // max(1, len(blocks) - 1), 0)),
        ],
        out_specs=pl.BlockSpec((nx, ty, nz), lambda i: (0, i, 0)),
        out_shape=jax.ShapeDtypeStruct((nx, ty * len(blocks), nz), jnp.float32),
        scratch_shapes=[pltpu.VMEM((nx + 2 * HW, ty, nz), jnp.float32)],
        cost_estimate=pl.CostEstimate(
            flops=40 * nx * ty * nz * len(blocks), transcendentals=0,
            bytes_accessed=int(nx * ty * nz * len(blocks) * 10),
        ),
    )(taps, raw, low, high)


def _y_kernel(taps_ref, first_ref, middle_ref, last_ref, low_ref, high_ref, out_ref, ext_ref):
    edge = first_ref.shape[1]
    ny = middle_ref.shape[1] + 2 * edge
    ext_ref[:, HW:2 * HW] = low_ref[...]
    ext_ref[:, 2 * HW:2 * HW + edge] = first_ref[...]
    ext_ref[:, 2 * HW + edge:2 * HW + ny - edge] = middle_ref[...]
    ext_ref[:, 2 * HW + ny - edge:2 * HW + ny] = last_ref[...]
    ext_ref[:, 2 * HW + ny:3 * HW + ny] = high_ref[...]
    out = taps_ref[0] * ext_ref[:, pl.ds(HW, ny)]
    for j in range(1, 2 * HW + 1):
        out = out + taps_ref[j] * ext_ref[:, pl.ds(HW + j, ny)]
    out_ref[...] = out


def smooth_y(edges, middle, low, high, taps, tx=4):
    nx, two_edge, nz = edges.shape
    edge = two_edge // 2
    ny = middle.shape[1] + two_edge
    return pl.pallas_call(
        _y_kernel,
        grid=(nx // tx,),
        in_specs=[
            pl.BlockSpec(memory_space=pltpu.SMEM),
            pl.BlockSpec((tx, edge, nz), lambda i: (i, 0, 0)),
            pl.BlockSpec((tx, ny - 2 * edge, nz), lambda i: (i, 0, 0)),
            pl.BlockSpec((tx, edge, nz), lambda i: (i, 1, 0)),
            pl.BlockSpec((tx, HW, nz), lambda i: (i, 0, 0)),
            pl.BlockSpec((tx, HW, nz), lambda i: (i, 0, 0)),
        ],
        out_specs=pl.BlockSpec((tx, ny, nz), lambda i: (i, 0, 0)),
        out_shape=jax.ShapeDtypeStruct((nx, ny, nz), jnp.float32),
        scratch_shapes=[pltpu.VMEM((tx, ny + 4 * HW, nz), jnp.float32)],
        cost_estimate=pl.CostEstimate(
            flops=18 * nx * ny * nz, transcendentals=0, bytes_accessed=int(nx * ny * nz * 8.8)
        ),
    )(taps, edges, middle, edges, low, high)


CHUNK = 128
HALO = 64


def halos(block, axis, dim, width):
    count = lax.axis_size(axis)
    forward = [(i, i + 1) for i in range(count - 1)]
    backward = [(target, source) for source, target in forward]
    low = lax.ppermute(
        lax.slice_in_dim(block, block.shape[dim] - width, None, axis=dim), axis, forward
    )
    high = lax.ppermute(lax.slice_in_dim(block, 0, width, axis=dim), axis, backward)
    return low, high


def extended(block, sides, width):
    for axis, dim in sides:
        count = lax.axis_size(axis)
        forward = [(i, i + 1) for i in range(count - 1)]
        backward = [(target, source) for source, target in forward]
        low = lax.ppermute(
            lax.slice_in_dim(block, block.shape[dim] - width, None, axis=dim), axis, forward
        )
        high = lax.ppermute(lax.slice_in_dim(block, 0, width, axis=dim), axis, backward)
        block = jnp.concatenate([low, block, high], axis=dim)
    return block


def band_block(values, centre):
    k = jnp.arange(CHUNK + 2 * HALO)[:, None]
    n = jnp.arange(CHUNK)[None, :]
    tap = k - n - HALO + centre
    block = jnp.zeros((CHUNK + 2 * HALO, CHUNK), jnp.float32)
    for j in range(values.shape[0]):
        block = jnp.where(tap == j, values[j], block)
    return block


def split(x):
    high = lax.reduce_precision(x, exponent_bits=8, mantissa_bits=7)
    return high.astype(jnp.bfloat16), (x - high).astype(jnp.bfloat16)


def windows(x):
    rows, length = x.shape
    chunks = length // CHUNK
    padded = jnp.pad(x, ((0, 0), (HALO, HALO)))
    pieces = padded.reshape(rows, chunks + 1, CHUNK)
    joined = jnp.concatenate([pieces[:, :chunks], pieces[:, 1:]], axis=-1)
    return joined.reshape(rows * chunks, CHUNK + 2 * HALO)


def banded(signal, block):
    rows, length = signal.shape
    x_high, x_low = split(signal)
    b_high, b_low = lax.optimization_barrier(split(block))
    w_high, w_low = windows(x_high), windows(x_low)
    out = (
        jnp.dot(w_high, b_high, preferred_element_type=jnp.float32)
        + jnp.dot(w_high, b_low, preferred_element_type=jnp.float32)
        + jnp.dot(w_low, b_high, preferred_element_type=jnp.float32)
    )
    return out.reshape(rows, length)


def filter_padded(padded, taps, axis):
    length = padded.shape[axis] - 8
    shape_out = list(padded.shape)
    shape_out[axis] = length
    result = jnp.zeros(tuple(shape_out), jnp.float32)
    for offset in range(9):
        result = result + taps[offset] * lax.slice_in_dim(
            padded, offset, offset + length, axis=axis
        )
    return result


def traverse(blocks):
    return lax.all_to_all(blocks, ("inline", "xline"), split_axis=0, concat_axis=0, tiled=True)


def local(image, weights, observed, wavelet, taps, aperture, landing):
    axes = ("inline", "xline")
    device_count = lax.axis_size("inline") * lax.axis_size("xline")
    me = lax.axis_index("inline") * lax.axis_size("xline") + lax.axis_index("xline")
    block_count, aperture_len = aperture.shape
    trace_count, samples = observed.shape
    per_block = trace_count // block_count
    rows_x, rows_y, depth_len = image.shape
    cell_count = rows_x * rows_y
    capacity = 2 * max(1, block_count * aperture_len // device_count)
    item_count = block_count * aperture_len
    tables = jnp.concatenate(
        [aperture, landing.reshape(block_count, per_block * aperture_len)], axis=1
    ).astype(jnp.float32)
    tables_all = jnp.round(lax.all_gather(tables, axes, axis=0, tiled=True))
    target_tile = aperture.reshape(item_count)
    onehot = (target_tile[:, None] == jnp.arange(device_count, dtype=jnp.int32)[None, :]).astype(
        jnp.int32
    )
    before = jnp.cumsum(onehot, axis=0) - onehot
    slot_index = jnp.sum(before * onehot, axis=1)
    target_slot = target_tile * capacity + slot_index
    item_cells = (
        landing.reshape(block_count, per_block, aperture_len)
        .transpose(0, 2, 1)
        .reshape(item_count, per_block)
    )
    cell_send = (
        jnp.zeros((device_count * capacity, per_block), jnp.int32).at[target_slot].set(item_cells)
    )
    cell_recv = lax.all_to_all(
        cell_send.reshape(device_count, capacity * per_block),
        axes,
        split_axis=0,
        concat_axis=0,
        tiled=True,
    )
    cell_recv = cell_recv.reshape(device_count * capacity * per_block)
    tile_rows = image.reshape(cell_count, depth_len)
    weight_matrix = weights.reshape(samples, depth_len)
    contract = (((1,), (1,)), ((), ()))
    half_cap = capacity // 2
    requests = cell_recv.reshape(device_count, capacity, per_block)
    returned = []
    for part in range(2):
        wanted = requests[:, part * half_cap:(part + 1) * half_cap].reshape(-1)
        predicted = lax.dot_general(
            jnp.take(tile_rows, wanted, axis=0), weight_matrix, contract,
            preferred_element_type=jnp.float32,
        ).astype(jnp.bfloat16)
        returned.append(
            traverse(predicted.reshape(device_count, half_cap * per_block, samples)).reshape(
                device_count * half_cap, per_block, samples
            )
        )
    tile_of = target_tile
    within = slot_index % half_cap
    from_first = jnp.take(returned[0], tile_of * half_cap + within, axis=0)
    from_second = jnp.take(returned[1], tile_of * half_cap + within, axis=0)
    own_preds = jnp.where(
        (slot_index < half_cap)[:, None, None], from_first, from_second
    ).reshape(block_count, aperture_len, per_block, samples)
    synthetic = jnp.sum(own_preds.astype(jnp.float32), axis=1).reshape(trace_count, samples)
    half = wavelet.shape[0] // 2
    modeled = banded(synthetic, band_block(wavelet[::-1], half))
    residual = modeled - observed.astype(jnp.float32)
    adjoint = banded(residual, band_block(wavelet, half)).astype(jnp.bfloat16)

    adjoint_all = lax.all_gather(adjoint, axes, axis=0, tiled=True)
    all_blocks = block_count * device_count
    aperture_all = tables_all[:, :aperture_len].astype(jnp.int32)
    landing_all = tables_all[:, aperture_len:].astype(jnp.int32).reshape(all_blocks * per_block, aperture_len)
    relevant = capacity * device_count
    hit = aperture_all == me
    has = jnp.any(hit, axis=1)
    entry = jnp.argmax(hit, axis=1).astype(jnp.int32)
    position = jnp.cumsum(has.astype(jnp.int32)) - 1
    slot = jnp.where(has, position, relevant)
    chosen = (
        jnp.zeros((relevant,), jnp.int32)
        .at[slot]
        .set(jnp.arange(all_blocks, dtype=jnp.int32), mode="drop")
    )
    found = jnp.sum(has.astype(jnp.int32))
    cells_all = jnp.take_along_axis(
        landing_all.reshape(all_blocks, per_block, aperture_len), entry[:, None, None], axis=2
    )[:, :, 0]
    cells = jnp.where(
        (jnp.arange(relevant) < found)[:, None], jnp.take(cells_all, chosen, axis=0), cell_count
    )
    picked = jnp.take(adjoint_all.reshape(all_blocks, per_block, samples), chosen, axis=0)
    weight_wide = jnp.pad(weight_matrix.astype(jnp.float32), ((0, 0), (HW, HW)))
    smoothed_weights = filter_padded(weight_wide, taps, 1)
    w_high, w_low = split(smoothed_weights)
    flat = picked.reshape(relevant * per_block, samples)
    per_trace = jnp.dot(flat, w_high, preferred_element_type=jnp.float32) + jnp.dot(
        flat, w_low, preferred_element_type=jnp.float32
    )
    raw_gradient = (
        jnp.zeros((cell_count, depth_len), jnp.float32)
        .at[cells.reshape(relevant * per_block)]
        .add(per_trace, mode="drop")
    )
    raw_gradient = raw_gradient.reshape(rows_x, rows_y, depth_len)
    raw_low, raw_high = halos(raw_gradient, "inline", 0, HW)
    y_blocks = rows_y // 8
    edges = smooth_zx(raw_gradient, raw_low, raw_high, taps, (0, y_blocks - 1))
    x_low, x_high = halos(edges, "xline", 1, HW)
    middle = smooth_zx(raw_gradient, raw_low, raw_high, taps, tuple(range(1, y_blocks - 1)))
    gradient = smooth_y(edges, middle, x_low, x_high, taps)
    return (gradient, residual)


def solution(mesh):
    return jax.shard_map(
        local,
        mesh=mesh,
        in_specs=(
            P("inline", "xline", None),
            P("inline", "xline", None, None),
            P(("inline", "xline"), None),
            P(),
            P(),
            P(("inline", "xline"), None),
            P(("inline", "xline"), None),
        ),
        out_specs=(P("inline", "xline", None), P(("inline", "xline"), None)),
        check_vma=False,
    )
```

```python
import jax
import jax.numpy as jnp
from jax import lax
from jax.experimental import pallas as pl
from jax.experimental.pallas import tpu as pltpu
from jax.sharding import PartitionSpec as P

HW = 4


def _zx_kernel(taps_ref, main_ref, low_ref, high_ref, out_ref, ext_ref):
    nx = main_ref.shape[0]
    ext_ref[0:HW] = low_ref[...]
    ext_ref[HW:HW + nx] = main_ref[...]
    ext_ref[HW + nx:] = high_ref[...]
    out = taps_ref[0] * ext_ref[0:nx]
    for j in range(1, 2 * HW + 1):
        out = out + taps_ref[j] * ext_ref[j:j + nx]
    out_ref[...] = out


def smooth_zx(raw, low, high, taps, blocks, ty=8):
    nx, ny, nz = raw.shape
    return pl.pallas_call(
        _zx_kernel,
        grid=(len(blocks),),
        in_specs=[
            pl.BlockSpec(memory_space=pltpu.SMEM),
            pl.BlockSpec((nx, ty, nz), lambda i: (0, blocks[0] + i * (blocks[-1] - blocks[0]) // max(1, len(blocks) - 1), 0)),
            pl.BlockSpec((HW, ty, nz), lambda i: (0, blocks[0] + i * (blocks[-1] - blocks[0]) // max(1, len(blocks) - 1), 0)),
            pl.BlockSpec((HW, ty, nz), lambda i: (0, blocks[0] + i * (blocks[-1] - blocks[0]) // max(1, len(blocks) - 1), 0)),
        ],
        out_specs=pl.BlockSpec((nx, ty, nz), lambda i: (0, i, 0)),
        out_shape=jax.ShapeDtypeStruct((nx, ty * len(blocks), nz), jnp.float32),
        scratch_shapes=[pltpu.VMEM((nx + 2 * HW, ty, nz), jnp.float32)],
        cost_estimate=pl.CostEstimate(
            flops=40 * nx * ty * nz * len(blocks), transcendentals=0,
            bytes_accessed=int(nx * ty * nz * len(blocks) * 10),
        ),
    )(taps, raw, low, high)


def _y_kernel(taps_ref, first_ref, middle_ref, last_ref, low_ref, high_ref, out_ref, ext_ref):
    edge = first_ref.shape[1]
    ny = middle_ref.shape[1] + 2 * edge
    ext_ref[:, HW:2 * HW] = low_ref[...]
    ext_ref[:, 2 * HW:2 * HW + edge] = first_ref[...]
    ext_ref[:, 2 * HW + edge:2 * HW + ny - edge] = middle_ref[...]
    ext_ref[:, 2 * HW + ny - edge:2 * HW + ny] = last_ref[...]
    ext_ref[:, 2 * HW + ny:3 * HW + ny] = high_ref[...]
    out = taps_ref[0] * ext_ref[:, pl.ds(HW, ny)]
    for j in range(1, 2 * HW + 1):
        out = out + taps_ref[j] * ext_ref[:, pl.ds(HW + j, ny)]
    out_ref[...] = out


def smooth_y(edges, middle, low, high, taps, tx=4):
    nx, two_edge, nz = edges.shape
    edge = two_edge // 2
    ny = middle.shape[1] + two_edge
    return pl.pallas_call(
        _y_kernel,
        grid=(nx // tx,),
        in_specs=[
            pl.BlockSpec(memory_space=pltpu.SMEM),
            pl.BlockSpec((tx, edge, nz), lambda i: (i, 0, 0)),
            pl.BlockSpec((tx, ny - 2 * edge, nz), lambda i: (i, 0, 0)),
            pl.BlockSpec((tx, edge, nz), lambda i: (i, 1, 0)),
            pl.BlockSpec((tx, HW, nz), lambda i: (i, 0, 0)),
            pl.BlockSpec((tx, HW, nz), lambda i: (i, 0, 0)),
        ],
        out_specs=pl.BlockSpec((tx, ny, nz), lambda i: (i, 0, 0)),
        out_shape=jax.ShapeDtypeStruct((nx, ny, nz), jnp.float32),
        scratch_shapes=[pltpu.VMEM((tx, ny + 4 * HW, nz), jnp.float32)],
        cost_estimate=pl.CostEstimate(
            flops=18 * nx * ny * nz, transcendentals=0, bytes_accessed=int(nx * ny * nz * 8.8)
        ),
    )(taps, edges, middle, edges, low, high)


CHUNK = 128
HALO = 64


def halos(block, axis, dim, width):
    count = lax.axis_size(axis)
    forward = [(i, i + 1) for i in range(count - 1)]
    backward = [(target, source) for source, target in forward]
    low = lax.ppermute(
        lax.slice_in_dim(block, block.shape[dim] - width, None, axis=dim), axis, forward
    )
    high = lax.ppermute(lax.slice_in_dim(block, 0, width, axis=dim), axis, backward)
    return low, high


def extended(block, sides, width):
    for axis, dim in sides:
        count = lax.axis_size(axis)
        forward = [(i, i + 1) for i in range(count - 1)]
        backward = [(target, source) for source, target in forward]
        low = lax.ppermute(
            lax.slice_in_dim(block, block.shape[dim] - width, None, axis=dim), axis, forward
        )
        high = lax.ppermute(lax.slice_in_dim(block, 0, width, axis=dim), axis, backward)
        block = jnp.concatenate([low, block, high], axis=dim)
    return block


def band_block(values, centre):
    k = jnp.arange(CHUNK + 2 * HALO)[:, None]
    n = jnp.arange(CHUNK)[None, :]
    tap = k - n - HALO + centre
    block = jnp.zeros((CHUNK + 2 * HALO, CHUNK), jnp.float32)
    for j in range(values.shape[0]):
        block = jnp.where(tap == j, values[j], block)
    return block


def split(x):
    high = lax.reduce_precision(x, exponent_bits=8, mantissa_bits=7)
    return high.astype(jnp.bfloat16), (x - high).astype(jnp.bfloat16)


def windows(x):
    rows, length = x.shape
    chunks = length // CHUNK
    padded = jnp.pad(x, ((0, 0), (HALO, HALO)))
    pieces = padded.reshape(rows, chunks + 1, CHUNK)
    joined = jnp.concatenate([pieces[:, :chunks], pieces[:, 1:]], axis=-1)
    return joined.reshape(rows * chunks, CHUNK + 2 * HALO)


def banded(signal, block):
    rows, length = signal.shape
    x_high, x_low = split(signal)
    b_high, b_low = lax.optimization_barrier(split(block))
    w_high, w_low = windows(x_high), windows(x_low)
    out = (
        jnp.dot(w_high, b_high, preferred_element_type=jnp.float32)
        + jnp.dot(w_high, b_low, preferred_element_type=jnp.float32)
        + jnp.dot(w_low, b_high, preferred_element_type=jnp.float32)
    )
    return out.reshape(rows, length)


def filter_padded(padded, taps, axis):
    length = padded.shape[axis] - 8
    shape_out = list(padded.shape)
    shape_out[axis] = length
    result = jnp.zeros(tuple(shape_out), jnp.float32)
    for offset in range(9):
        result = result + taps[offset] * lax.slice_in_dim(
            padded, offset, offset + length, axis=axis
        )
    return result


def traverse(blocks):
    return lax.all_to_all(blocks, ("inline", "xline"), split_axis=0, concat_axis=0, tiled=True)


def local(image, weights, observed, wavelet, taps, aperture, landing):
    axes = ("inline", "xline")
    device_count = lax.axis_size("inline") * lax.axis_size("xline")
    me = lax.axis_index("inline") * lax.axis_size("xline") + lax.axis_index("xline")
    block_count, aperture_len = aperture.shape
    trace_count, samples = observed.shape
    per_block = trace_count // block_count
    rows_x, rows_y, depth_len = image.shape
    cell_count = rows_x * rows_y
    capacity = 2 * max(1, block_count * aperture_len // device_count)
    item_count = block_count * aperture_len
    tables = jnp.concatenate(
        [aperture, landing.reshape(block_count, per_block * aperture_len)], axis=1
    ).astype(jnp.float32)
    tables_all = jnp.round(lax.all_gather(tables, axes, axis=0, tiled=True))
    target_tile = aperture.reshape(item_count)
    onehot = (target_tile[:, None] == jnp.arange(device_count, dtype=jnp.int32)[None, :]).astype(
        jnp.int32
    )
    before = jnp.cumsum(onehot, axis=0) - onehot
    slot_index = jnp.sum(before * onehot, axis=1)
    target_slot = target_tile * capacity + slot_index
    item_cells = (
        landing.reshape(block_count, per_block, aperture_len)
        .transpose(0, 2, 1)
        .reshape(item_count, per_block)
    )
    cell_send = (
        jnp.zeros((device_count * capacity, per_block), jnp.int32).at[target_slot].set(item_cells)
    )
    cell_recv = lax.all_to_all(
        cell_send.reshape(device_count, capacity * per_block),
        axes,
        split_axis=0,
        concat_axis=0,
        tiled=True,
    )
    cell_recv = cell_recv.reshape(device_count * capacity * per_block)
    tile_rows = image.reshape(cell_count, depth_len)
    weight_matrix = weights.reshape(samples, depth_len)
    contract = (((1,), (1,)), ((), ()))
    half_cap = capacity // 2
    requests = cell_recv.reshape(device_count, capacity, per_block)
    returned = []
    for part in range(2):
        wanted = requests[:, part * half_cap:(part + 1) * half_cap].reshape(-1)
        predicted = lax.dot_general(
            jnp.take(tile_rows, wanted, axis=0), weight_matrix, contract,
            preferred_element_type=jnp.float32,
        ).astype(jnp.bfloat16)
        returned.append(
            traverse(predicted.reshape(device_count, half_cap * per_block, samples)).reshape(
                device_count * half_cap, per_block, samples
            )
        )
    tile_of = target_tile
    within = slot_index % half_cap
    from_first = jnp.take(returned[0], tile_of * half_cap + within, axis=0)
    from_second = jnp.take(returned[1], tile_of * half_cap + within, axis=0)
    own_preds = jnp.where(
        (slot_index < half_cap)[:, None, None], from_first, from_second
    ).reshape(block_count, aperture_len, per_block, samples)
    synthetic = jnp.sum(own_preds.astype(jnp.float32), axis=1).reshape(trace_count, samples)
    half = wavelet.shape[0] // 2
    modeled = banded(synthetic, band_block(wavelet[::-1], half))
    residual = modeled - observed.astype(jnp.float32)
    adjoint = banded(residual, band_block(wavelet, half)).astype(jnp.bfloat16)

    adjoint_all = lax.all_gather(adjoint, axes, axis=0, tiled=True)
    all_blocks = block_count * device_count
    aperture_all = tables_all[:, :aperture_len].astype(jnp.int32)
    landing_all = tables_all[:, aperture_len:].astype(jnp.int32).reshape(all_blocks * per_block, aperture_len)
    relevant = capacity * device_count
    hit = aperture_all == me
    has = jnp.any(hit, axis=1)
    entry = jnp.argmax(hit, axis=1).astype(jnp.int32)
    position = jnp.cumsum(has.astype(jnp.int32)) - 1
    slot = jnp.where(has, position, relevant)
    chosen = (
        jnp.zeros((relevant,), jnp.int32)
        .at[slot]
        .set(jnp.arange(all_blocks, dtype=jnp.int32), mode="drop")
    )
    found = jnp.sum(has.astype(jnp.int32))
    cells_all = jnp.take_along_axis(
        landing_all.reshape(all_blocks, per_block, aperture_len), entry[:, None, None], axis=2
    )[:, :, 0]
    cells = jnp.where(
        (jnp.arange(relevant) < found)[:, None], jnp.take(cells_all, chosen, axis=0), cell_count
    )
    picked = jnp.take(adjoint_all.reshape(all_blocks, per_block, samples), chosen, axis=0)
    weight_wide = jnp.pad(weight_matrix.astype(jnp.float32), ((0, 0), (HW, HW)))
    smoothed_weights = filter_padded(weight_wide, taps, 1)
    flat = picked.reshape(relevant * per_block, samples)
    per_trace = jnp.dot(
        flat, smoothed_weights.astype(jnp.bfloat16), preferred_element_type=jnp.float32
    )
    raw_gradient = (
        jnp.zeros((cell_count, depth_len), jnp.float32)
        .at[cells.reshape(relevant * per_block)]
        .add(per_trace, mode="drop")
    )
    raw_gradient = raw_gradient.reshape(rows_x, rows_y, depth_len)
    raw_low, raw_high = halos(raw_gradient, "inline", 0, HW)
    y_blocks = rows_y // 8
    edges = smooth_zx(raw_gradient, raw_low, raw_high, taps, (0, y_blocks - 1))
    x_low, x_high = halos(edges, "xline", 1, HW)
    middle = smooth_zx(raw_gradient, raw_low, raw_high, taps, tuple(range(1, y_blocks - 1)))
    gradient = smooth_y(edges, middle, x_low, x_high, taps)
    return (gradient, residual)


def solution(mesh):
    return jax.shard_map(
        local,
        mesh=mesh,
        in_specs=(
            P("inline", "xline", None),
            P("inline", "xline", None, None),
            P(("inline", "xline"), None),
            P(),
            P(),
            P(("inline", "xline"), None),
            P(("inline", "xline"), None),
        ),
        out_specs=(P("inline", "xline", None), P(("inline", "xline"), None)),
        check_vma=False,
    )
```

```python
import jax
import jax.numpy as jnp
from jax import lax
from jax.experimental import pallas as pl
from jax.experimental.pallas import tpu as pltpu
from jax.sharding import PartitionSpec as P

HW = 4


def _zx_kernel(taps_ref, main_ref, low_ref, high_ref, out_ref, ext_ref):
    nx = main_ref.shape[0]
    ext_ref[0:HW] = low_ref[...]
    ext_ref[HW:HW + nx] = main_ref[...]
    ext_ref[HW + nx:] = high_ref[...]
    lanes = 128

    def lane_chunk(c, carry):
        cols = pl.ds(pl.multiple_of(c * lanes, lanes), lanes)
        out = taps_ref[0] * ext_ref[0:nx, :, cols]
        for j in range(1, 2 * HW + 1):
            out = out + taps_ref[j] * ext_ref[j:j + nx, :, cols]
        out_ref[:, :, cols] = out
        return carry

    lax.fori_loop(0, main_ref.shape[2] // lanes, lane_chunk, 0)


def smooth_zx(raw, low, high, taps, blocks, ty=8):
    nx, ny, nz = raw.shape
    return pl.pallas_call(
        _zx_kernel,
        grid=(len(blocks),),
        in_specs=[
            pl.BlockSpec(memory_space=pltpu.SMEM),
            pl.BlockSpec((nx, ty, nz), lambda i: (0, blocks[0] + i * (blocks[-1] - blocks[0]) // max(1, len(blocks) - 1), 0)),
            pl.BlockSpec((HW, ty, nz), lambda i: (0, blocks[0] + i * (blocks[-1] - blocks[0]) // max(1, len(blocks) - 1), 0)),
            pl.BlockSpec((HW, ty, nz), lambda i: (0, blocks[0] + i * (blocks[-1] - blocks[0]) // max(1, len(blocks) - 1), 0)),
        ],
        out_specs=pl.BlockSpec((nx, ty, nz), lambda i: (0, i, 0)),
        out_shape=jax.ShapeDtypeStruct((nx, ty * len(blocks), nz), jnp.float32),
        scratch_shapes=[pltpu.VMEM((nx + 2 * HW, ty, nz), jnp.float32)],
        cost_estimate=pl.CostEstimate(
            flops=40 * nx * ty * nz * len(blocks), transcendentals=0,
            bytes_accessed=int(nx * ty * nz * len(blocks) * 10),
        ),
    )(taps, raw, low, high)


def _y_kernel(taps_ref, first_ref, middle_ref, last_ref, low_ref, high_ref, out_ref, ext_ref):
    edge = first_ref.shape[1]
    ny = middle_ref.shape[1] + 2 * edge
    ext_ref[:, HW:2 * HW] = low_ref[...]
    ext_ref[:, 2 * HW:2 * HW + edge] = first_ref[...]
    ext_ref[:, 2 * HW + edge:2 * HW + ny - edge] = middle_ref[...]
    ext_ref[:, 2 * HW + ny - edge:2 * HW + ny] = last_ref[...]
    ext_ref[:, 2 * HW + ny:3 * HW + ny] = high_ref[...]
    lanes = 128

    def lane_chunk(c, carry):
        cols = pl.ds(pl.multiple_of(c * lanes, lanes), lanes)
        out = taps_ref[0] * ext_ref[:, pl.ds(HW, ny), cols]
        for j in range(1, 2 * HW + 1):
            out = out + taps_ref[j] * ext_ref[:, pl.ds(HW + j, ny), cols]
        out_ref[:, :, cols] = out
        return carry

    lax.fori_loop(0, out_ref.shape[2] // lanes, lane_chunk, 0)


def smooth_y(edges, middle, low, high, taps, tx=4):
    nx, two_edge, nz = edges.shape
    edge = two_edge // 2
    ny = middle.shape[1] + two_edge
    return pl.pallas_call(
        _y_kernel,
        grid=(nx // tx,),
        in_specs=[
            pl.BlockSpec(memory_space=pltpu.SMEM),
            pl.BlockSpec((tx, edge, nz), lambda i: (i, 0, 0)),
            pl.BlockSpec((tx, ny - 2 * edge, nz), lambda i: (i, 0, 0)),
            pl.BlockSpec((tx, edge, nz), lambda i: (i, 1, 0)),
            pl.BlockSpec((tx, HW, nz), lambda i: (i, 0, 0)),
            pl.BlockSpec((tx, HW, nz), lambda i: (i, 0, 0)),
        ],
        out_specs=pl.BlockSpec((tx, ny, nz), lambda i: (i, 0, 0)),
        out_shape=jax.ShapeDtypeStruct((nx, ny, nz), jnp.float32),
        scratch_shapes=[pltpu.VMEM((tx, ny + 4 * HW, nz), jnp.float32)],
        cost_estimate=pl.CostEstimate(
            flops=18 * nx * ny * nz, transcendentals=0, bytes_accessed=int(nx * ny * nz * 8.8)
        ),
    )(taps, edges, middle, edges, low, high)


CHUNK = 128
HALO = 64


def halos(block, axis, dim, width):
    count = lax.axis_size(axis)
    forward = [(i, i + 1) for i in range(count - 1)]
    backward = [(target, source) for source, target in forward]
    low = lax.ppermute(
        lax.slice_in_dim(block, block.shape[dim] - width, None, axis=dim), axis, forward
    )
    high = lax.ppermute(lax.slice_in_dim(block, 0, width, axis=dim), axis, backward)
    return low, high


def extended(block, sides, width):
    for axis, dim in sides:
        count = lax.axis_size(axis)
        forward = [(i, i + 1) for i in range(count - 1)]
        backward = [(target, source) for source, target in forward]
        low = lax.ppermute(
            lax.slice_in_dim(block, block.shape[dim] - width, None, axis=dim), axis, forward
        )
        high = lax.ppermute(lax.slice_in_dim(block, 0, width, axis=dim), axis, backward)
        block = jnp.concatenate([low, block, high], axis=dim)
    return block


def band_block(values, centre):
    k = jnp.arange(CHUNK + 2 * HALO)[:, None]
    n = jnp.arange(CHUNK)[None, :]
    tap = k - n - HALO + centre
    block = jnp.zeros((CHUNK + 2 * HALO, CHUNK), jnp.float32)
    for j in range(values.shape[0]):
        block = jnp.where(tap == j, values[j], block)
    return block


def split(x):
    high = lax.reduce_precision(x, exponent_bits=8, mantissa_bits=7)
    return high.astype(jnp.bfloat16), (x - high).astype(jnp.bfloat16)


def windows(x):
    rows, length = x.shape
    chunks = length // CHUNK
    padded = jnp.pad(x, ((0, 0), (HALO, HALO)))
    pieces = padded.reshape(rows, chunks + 1, CHUNK)
    joined = jnp.concatenate([pieces[:, :chunks], pieces[:, 1:]], axis=-1)
    return joined.reshape(rows * chunks, CHUNK + 2 * HALO)


def banded(signal, block):
    rows, length = signal.shape
    x_high, x_low = split(signal)
    b_high, b_low = lax.optimization_barrier(split(block))
    w_high, w_low = windows(x_high), windows(x_low)
    out = (
        jnp.dot(w_high, b_high, preferred_element_type=jnp.float32)
        + jnp.dot(w_high, b_low, preferred_element_type=jnp.float32)
        + jnp.dot(w_low, b_high, preferred_element_type=jnp.float32)
    )
    return out.reshape(rows, length)


def filter_padded(padded, taps, axis):
    length = padded.shape[axis] - 8
    shape_out = list(padded.shape)
    shape_out[axis] = length
    result = jnp.zeros(tuple(shape_out), jnp.float32)
    for offset in range(9):
        result = result + taps[offset] * lax.slice_in_dim(
            padded, offset, offset + length, axis=axis
        )
    return result


def traverse(blocks):
    return lax.all_to_all(blocks, ("inline", "xline"), split_axis=0, concat_axis=0, tiled=True)


def local(image, weights, observed, wavelet, taps, aperture, landing):
    axes = ("inline", "xline")
    device_count = lax.axis_size("inline") * lax.axis_size("xline")
    me = lax.axis_index("inline") * lax.axis_size("xline") + lax.axis_index("xline")
    block_count, aperture_len = aperture.shape
    trace_count, samples = observed.shape
    per_block = trace_count // block_count
    rows_x, rows_y, depth_len = image.shape
    cell_count = rows_x * rows_y
    capacity = 2 * max(1, block_count * aperture_len // device_count)
    item_count = block_count * aperture_len
    tables = jnp.concatenate(
        [aperture, landing.reshape(block_count, per_block * aperture_len)], axis=1
    ).astype(jnp.float32)
    tables_all = jnp.round(lax.all_gather(tables, axes, axis=0, tiled=True))
    target_tile = aperture.reshape(item_count)
    onehot = (target_tile[:, None] == jnp.arange(device_count, dtype=jnp.int32)[None, :]).astype(
        jnp.int32
    )
    before = jnp.cumsum(onehot, axis=0) - onehot
    slot_index = jnp.sum(before * onehot, axis=1)
    target_slot = target_tile * capacity + slot_index
    item_cells = (
        landing.reshape(block_count, per_block, aperture_len)
        .transpose(0, 2, 1)
        .reshape(item_count, per_block)
    )
    cell_send = (
        jnp.zeros((device_count * capacity, per_block), jnp.int32).at[target_slot].set(item_cells)
    )
    cell_recv = lax.all_to_all(
        cell_send.reshape(device_count, capacity * per_block),
        axes,
        split_axis=0,
        concat_axis=0,
        tiled=True,
    )
    cell_recv = cell_recv.reshape(device_count * capacity * per_block)
    tile_rows = image.reshape(cell_count, depth_len)
    weight_matrix = weights.reshape(samples, depth_len)
    contract = (((1,), (1,)), ((), ()))
    half_cap = capacity // 2
    requests = cell_recv.reshape(device_count, capacity, per_block)
    returned = []
    for part in range(2):
        wanted = requests[:, part * half_cap:(part + 1) * half_cap].reshape(-1)
        predicted = lax.dot_general(
            jnp.take(tile_rows, wanted, axis=0), weight_matrix, contract,
            preferred_element_type=jnp.float32,
        ).astype(jnp.bfloat16)
        returned.append(
            traverse(predicted.reshape(device_count, half_cap * per_block, samples)).reshape(
                device_count * half_cap, per_block, samples
            )
        )
    tile_of = target_tile
    within = slot_index % half_cap
    from_first = jnp.take(returned[0], tile_of * half_cap + within, axis=0)
    from_second = jnp.take(returned[1], tile_of * half_cap + within, axis=0)
    own_preds = jnp.where(
        (slot_index < half_cap)[:, None, None], from_first, from_second
    ).reshape(block_count, aperture_len, per_block, samples)
    synthetic = jnp.sum(own_preds.astype(jnp.float32), axis=1).reshape(trace_count, samples)
    half = wavelet.shape[0] // 2
    modeled = banded(synthetic, band_block(wavelet[::-1], half))
    residual = modeled - observed.astype(jnp.float32)
    adjoint = banded(residual, band_block(wavelet, half)).astype(jnp.bfloat16)

    adjoint_all = lax.all_gather(adjoint, axes, axis=0, tiled=True)
    all_blocks = block_count * device_count
    aperture_all = tables_all[:, :aperture_len].astype(jnp.int32)
    landing_all = tables_all[:, aperture_len:].astype(jnp.int32).reshape(all_blocks * per_block, aperture_len)
    relevant = capacity * device_count
    hit = aperture_all == me
    has = jnp.any(hit, axis=1)
    entry = jnp.argmax(hit, axis=1).astype(jnp.int32)
    position = jnp.cumsum(has.astype(jnp.int32)) - 1
    slot = jnp.where(has, position, relevant)
    chosen = (
        jnp.zeros((relevant,), jnp.int32)
        .at[slot]
        .set(jnp.arange(all_blocks, dtype=jnp.int32), mode="drop")
    )
    found = jnp.sum(has.astype(jnp.int32))
    cells_all = jnp.take_along_axis(
        landing_all.reshape(all_blocks, per_block, aperture_len), entry[:, None, None], axis=2
    )[:, :, 0]
    cells = jnp.where(
        (jnp.arange(relevant) < found)[:, None], jnp.take(cells_all, chosen, axis=0), cell_count
    )
    picked = jnp.take(adjoint_all.reshape(all_blocks, per_block, samples), chosen, axis=0)
    weight_wide = jnp.pad(weight_matrix.astype(jnp.float32), ((0, 0), (HW, HW)))
    smoothed_weights = filter_padded(weight_wide, taps, 1)
    w_high, w_low = split(smoothed_weights)
    flat = picked.reshape(relevant * per_block, samples)
    per_trace = jnp.dot(flat, w_high, preferred_element_type=jnp.float32) + jnp.dot(
        flat, w_low, preferred_element_type=jnp.float32
    )
    raw_gradient = (
        jnp.zeros((cell_count, depth_len), jnp.float32)
        .at[cells.reshape(relevant * per_block)]
        .add(per_trace, mode="drop")
    )
    raw_gradient = raw_gradient.reshape(rows_x, rows_y, depth_len)
    raw_low, raw_high = halos(raw_gradient, "inline", 0, HW)
    y_blocks = rows_y // 8
    edges = smooth_zx(raw_gradient, raw_low, raw_high, taps, (0, y_blocks - 1))
    x_low, x_high = halos(edges, "xline", 1, HW)
    middle = smooth_zx(raw_gradient, raw_low, raw_high, taps, tuple(range(1, y_blocks - 1)))
    gradient = smooth_y(edges, middle, x_low, x_high, taps)
    return (gradient, residual)


def solution(mesh):
    return jax.shard_map(
        local,
        mesh=mesh,
        in_specs=(
            P("inline", "xline", None),
            P("inline", "xline", None, None),
            P(("inline", "xline"), None),
            P(),
            P(),
            P(("inline", "xline"), None),
            P(("inline", "xline"), None),
        ),
        out_specs=(P("inline", "xline", None), P(("inline", "xline"), None)),
        check_vma=False,
    )
```

```python
import jax
import jax.numpy as jnp
from jax import lax
from jax.experimental import pallas as pl
from jax.experimental.pallas import tpu as pltpu
from jax.sharding import PartitionSpec as P

HW = 4


def _zx_kernel(taps_ref, main_ref, low_ref, high_ref, out_ref, ext_ref):
    nx = main_ref.shape[0]
    ext_ref[0:HW] = low_ref[...]
    ext_ref[HW:HW + nx] = main_ref[...]
    ext_ref[HW + nx:] = high_ref[...]
    lanes = 128

    def lane_chunk(c, carry):
        cols = pl.ds(pl.multiple_of(c * lanes, lanes), lanes)
        out = taps_ref[0] * ext_ref[0:nx, :, cols]
        for j in range(1, 2 * HW + 1):
            out = out + taps_ref[j] * ext_ref[j:j + nx, :, cols]
        out_ref[:, :, cols] = out
        return carry

    lax.fori_loop(0, main_ref.shape[2] // lanes, lane_chunk, 0)


def smooth_zx(raw, low, high, taps, blocks, ty=8):
    nx, ny, nz = raw.shape
    return pl.pallas_call(
        _zx_kernel,
        grid=(len(blocks),),
        in_specs=[
            pl.BlockSpec(memory_space=pltpu.SMEM),
            pl.BlockSpec((nx, ty, nz), lambda i: (0, blocks[0] + i * (blocks[-1] - blocks[0]) // max(1, len(blocks) - 1), 0)),
            pl.BlockSpec((HW, ty, nz), lambda i: (0, blocks[0] + i * (blocks[-1] - blocks[0]) // max(1, len(blocks) - 1), 0)),
            pl.BlockSpec((HW, ty, nz), lambda i: (0, blocks[0] + i * (blocks[-1] - blocks[0]) // max(1, len(blocks) - 1), 0)),
        ],
        out_specs=pl.BlockSpec((nx, ty, nz), lambda i: (0, i, 0)),
        out_shape=jax.ShapeDtypeStruct((nx, ty * len(blocks), nz), jnp.float32),
        scratch_shapes=[pltpu.VMEM((nx + 2 * HW, ty, nz), jnp.float32)],
        cost_estimate=pl.CostEstimate(
            flops=40 * nx * ty * nz * len(blocks), transcendentals=0,
            bytes_accessed=int(nx * ty * nz * len(blocks) * 10),
        ),
    )(taps, raw, low, high)


def _y_kernel(taps_ref, first_ref, middle_ref, last_ref, low_ref, high_ref, out_ref, ext_ref):
    edge = first_ref.shape[1]
    ny = middle_ref.shape[1] + 2 * edge
    ext_ref[:, HW:2 * HW] = low_ref[...]
    ext_ref[:, 2 * HW:2 * HW + edge] = first_ref[...]
    ext_ref[:, 2 * HW + edge:2 * HW + ny - edge] = middle_ref[...]
    ext_ref[:, 2 * HW + ny - edge:2 * HW + ny] = last_ref[...]
    ext_ref[:, 2 * HW + ny:3 * HW + ny] = high_ref[...]
    lanes = 128

    def lane_chunk(c, carry):
        cols = pl.ds(pl.multiple_of(c * lanes, lanes), lanes)
        out = taps_ref[0] * ext_ref[:, pl.ds(HW, ny), cols]
        for j in range(1, 2 * HW + 1):
            out = out + taps_ref[j] * ext_ref[:, pl.ds(HW + j, ny), cols]
        out_ref[:, :, cols] = out
        return carry

    lax.fori_loop(0, out_ref.shape[2] // lanes, lane_chunk, 0)


def smooth_y(edges, middle, low, high, taps, tx=4):
    nx, two_edge, nz = edges.shape
    edge = two_edge // 2
    ny = middle.shape[1] + two_edge
    return pl.pallas_call(
        _y_kernel,
        grid=(nx // tx,),
        in_specs=[
            pl.BlockSpec(memory_space=pltpu.SMEM),
            pl.BlockSpec((tx, edge, nz), lambda i: (i, 0, 0)),
            pl.BlockSpec((tx, ny - 2 * edge, nz), lambda i: (i, 0, 0)),
            pl.BlockSpec((tx, edge, nz), lambda i: (i, 1, 0)),
            pl.BlockSpec((tx, HW, nz), lambda i: (i, 0, 0)),
            pl.BlockSpec((tx, HW, nz), lambda i: (i, 0, 0)),
        ],
        out_specs=pl.BlockSpec((tx, ny, nz), lambda i: (i, 0, 0)),
        out_shape=jax.ShapeDtypeStruct((nx, ny, nz), jnp.float32),
        scratch_shapes=[pltpu.VMEM((tx, ny + 4 * HW, nz), jnp.float32)],
        cost_estimate=pl.CostEstimate(
            flops=18 * nx * ny * nz, transcendentals=0, bytes_accessed=int(nx * ny * nz * 8.8)
        ),
    )(taps, edges, middle, edges, low, high)


CHUNK = 128
HALO = 64


def halos(block, axis, dim, width):
    count = lax.axis_size(axis)
    forward = [(i, i + 1) for i in range(count - 1)]
    backward = [(target, source) for source, target in forward]
    low = lax.ppermute(
        lax.slice_in_dim(block, block.shape[dim] - width, None, axis=dim), axis, forward
    )
    high = lax.ppermute(lax.slice_in_dim(block, 0, width, axis=dim), axis, backward)
    return low, high


def extended(block, sides, width):
    for axis, dim in sides:
        count = lax.axis_size(axis)
        forward = [(i, i + 1) for i in range(count - 1)]
        backward = [(target, source) for source, target in forward]
        low = lax.ppermute(
            lax.slice_in_dim(block, block.shape[dim] - width, None, axis=dim), axis, forward
        )
        high = lax.ppermute(lax.slice_in_dim(block, 0, width, axis=dim), axis, backward)
        block = jnp.concatenate([low, block, high], axis=dim)
    return block


def band_block(values, centre):
    k = jnp.arange(CHUNK + 2 * HALO)[:, None]
    n = jnp.arange(CHUNK)[None, :]
    tap = k - n - HALO + centre
    block = jnp.zeros((CHUNK + 2 * HALO, CHUNK), jnp.float32)
    for j in range(values.shape[0]):
        block = jnp.where(tap == j, values[j], block)
    return block


def split(x):
    high = lax.reduce_precision(x, exponent_bits=8, mantissa_bits=7)
    return high.astype(jnp.bfloat16), (x - high).astype(jnp.bfloat16)


def windows(x):
    rows, length = x.shape
    chunks = length // CHUNK
    padded = jnp.pad(x, ((0, 0), (HALO, HALO)))
    pieces = padded.reshape(rows, chunks + 1, CHUNK)
    joined = jnp.concatenate([pieces[:, :chunks], pieces[:, 1:]], axis=-1)
    return joined.reshape(rows * chunks, CHUNK + 2 * HALO)


def banded(signal, block):
    rows, length = signal.shape
    x_high, x_low = split(signal)
    b_high, b_low = lax.optimization_barrier(split(block))
    w_high, w_low = windows(x_high), windows(x_low)
    out = (
        jnp.dot(w_high, b_high, preferred_element_type=jnp.float32)
        + jnp.dot(w_high, b_low, preferred_element_type=jnp.float32)
        + jnp.dot(w_low, b_high, preferred_element_type=jnp.float32)
    )
    return out.reshape(rows, length)


def filter_padded(padded, taps, axis):
    length = padded.shape[axis] - 8
    shape_out = list(padded.shape)
    shape_out[axis] = length
    result = jnp.zeros(tuple(shape_out), jnp.float32)
    for offset in range(9):
        result = result + taps[offset] * lax.slice_in_dim(
            padded, offset, offset + length, axis=axis
        )
    return result


def traverse(blocks):
    return lax.all_to_all(blocks, ("inline", "xline"), split_axis=0, concat_axis=0, tiled=True)


def local(image, weights, observed, wavelet, taps, aperture, landing):
    axes = ("inline", "xline")
    device_count = lax.axis_size("inline") * lax.axis_size("xline")
    me = lax.axis_index("inline") * lax.axis_size("xline") + lax.axis_index("xline")
    block_count, aperture_len = aperture.shape
    trace_count, samples = observed.shape
    per_block = trace_count // block_count
    rows_x, rows_y, depth_len = image.shape
    cell_count = rows_x * rows_y
    capacity = 2 * max(1, block_count * aperture_len // device_count)
    item_count = block_count * aperture_len
    tables = jnp.concatenate(
        [aperture, landing.reshape(block_count, per_block * aperture_len)], axis=1
    ).astype(jnp.float32)
    target_tile = aperture.reshape(item_count)
    onehot = (target_tile[:, None] == jnp.arange(device_count, dtype=jnp.int32)[None, :]).astype(
        jnp.int32
    )
    before = jnp.cumsum(onehot, axis=0) - onehot
    slot_index = jnp.sum(before * onehot, axis=1)
    target_slot = target_tile * capacity + slot_index
    item_cells = (
        landing.reshape(block_count, per_block, aperture_len)
        .transpose(0, 2, 1)
        .reshape(item_count, per_block)
    )
    cell_send = (
        jnp.zeros((device_count * capacity, per_block), jnp.int32).at[target_slot].set(item_cells)
    )
    cell_recv = lax.all_to_all(
        cell_send.reshape(device_count, capacity * per_block),
        axes,
        split_axis=0,
        concat_axis=0,
        tiled=True,
    )
    cell_recv = cell_recv.reshape(device_count * capacity * per_block)
    tile_rows = image.reshape(cell_count, depth_len)
    weight_matrix = weights.reshape(samples, depth_len)
    contract = (((1,), (1,)), ((), ()))
    half_cap = capacity // 2
    requests = cell_recv.reshape(device_count, capacity, per_block)
    returned = []
    for part in range(2):
        wanted = requests[:, part * half_cap:(part + 1) * half_cap].reshape(-1)
        predicted = lax.dot_general(
            jnp.take(tile_rows, wanted, axis=0), weight_matrix, contract,
            preferred_element_type=jnp.float32,
        ).astype(jnp.bfloat16)
        if part == 0:
            predicted, late_tables = lax.optimization_barrier((predicted, tables))
            tables_all = jnp.round(lax.all_gather(late_tables, axes, axis=0, tiled=True))
        if part == 1:
            predicted, tables_all = lax.optimization_barrier((predicted, tables_all))
        returned.append(
            traverse(predicted.reshape(device_count, half_cap * per_block, samples)).reshape(
                device_count * half_cap, per_block, samples
            )
        )
    tile_of = target_tile
    within = slot_index % half_cap
    from_first = jnp.take(returned[0], tile_of * half_cap + within, axis=0)
    from_second = jnp.take(returned[1], tile_of * half_cap + within, axis=0)
    own_preds = jnp.where(
        (slot_index < half_cap)[:, None, None], from_first, from_second
    ).reshape(block_count, aperture_len, per_block, samples)
    synthetic = jnp.sum(own_preds.astype(jnp.float32), axis=1).reshape(trace_count, samples)
    half = wavelet.shape[0] // 2
    modeled = banded(synthetic, band_block(wavelet[::-1], half))
    residual = modeled - observed.astype(jnp.float32)
    adjoint = banded(residual, band_block(wavelet, half)).astype(jnp.bfloat16)

    adjoint_all = lax.all_gather(adjoint, axes, axis=0, tiled=True)
    all_blocks = block_count * device_count
    aperture_all = tables_all[:, :aperture_len].astype(jnp.int32)
    landing_all = tables_all[:, aperture_len:].astype(jnp.int32).reshape(all_blocks * per_block, aperture_len)
    relevant = capacity * device_count
    hit = aperture_all == me
    has = jnp.any(hit, axis=1)
    entry = jnp.argmax(hit, axis=1).astype(jnp.int32)
    position = jnp.cumsum(has.astype(jnp.int32)) - 1
    slot = jnp.where(has, position, relevant)
    chosen = (
        jnp.zeros((relevant,), jnp.int32)
        .at[slot]
        .set(jnp.arange(all_blocks, dtype=jnp.int32), mode="drop")
    )
    found = jnp.sum(has.astype(jnp.int32))
    cells_all = jnp.take_along_axis(
        landing_all.reshape(all_blocks, per_block, aperture_len), entry[:, None, None], axis=2
    )[:, :, 0]
    cells = jnp.where(
        (jnp.arange(relevant) < found)[:, None], jnp.take(cells_all, chosen, axis=0), cell_count
    )
    picked = jnp.take(adjoint_all.reshape(all_blocks, per_block, samples), chosen, axis=0)
    weight_wide = jnp.pad(weight_matrix.astype(jnp.float32), ((0, 0), (HW, HW)))
    smoothed_weights = filter_padded(weight_wide, taps, 1)
    w_high, w_low = split(smoothed_weights)
    flat = picked.reshape(relevant * per_block, samples)
    per_trace = jnp.dot(flat, w_high, preferred_element_type=jnp.float32) + jnp.dot(
        flat, w_low, preferred_element_type=jnp.float32
    )
    raw_gradient = (
        jnp.zeros((cell_count, depth_len), jnp.float32)
        .at[cells.reshape(relevant * per_block)]
        .add(per_trace, mode="drop")
    )
    raw_gradient = raw_gradient.reshape(rows_x, rows_y, depth_len)
    raw_low, raw_high = halos(raw_gradient, "inline", 0, HW)
    y_blocks = rows_y // 8
    edges = smooth_zx(raw_gradient, raw_low, raw_high, taps, (0, y_blocks - 1))
    x_low, x_high = halos(edges, "xline", 1, HW)
    middle = smooth_zx(raw_gradient, raw_low, raw_high, taps, tuple(range(1, y_blocks - 1)))
    gradient = smooth_y(edges, middle, x_low, x_high, taps)
    return (gradient, residual)


def solution(mesh):
    return jax.shard_map(
        local,
        mesh=mesh,
        in_specs=(
            P("inline", "xline", None),
            P("inline", "xline", None, None),
            P(("inline", "xline"), None),
            P(),
            P(),
            P(("inline", "xline"), None),
            P(("inline", "xline"), None),
        ),
        out_specs=(P("inline", "xline", None), P(("inline", "xline"), None)),
        check_vma=False,
    )
```

```python
import jax
import jax.numpy as jnp
from jax import lax
from jax.experimental import pallas as pl
from jax.experimental.pallas import tpu as pltpu
from jax.sharding import PartitionSpec as P

HW = 4


def _zx_kernel(taps_ref, main_ref, low_ref, high_ref, out_ref, ext_ref):
    nx = main_ref.shape[0]
    ext_ref[0:HW] = low_ref[...]
    ext_ref[HW:HW + nx] = main_ref[...]
    ext_ref[HW + nx:] = high_ref[...]
    lanes = 128

    def lane_chunk(c, carry):
        cols = pl.ds(pl.multiple_of(c * lanes, lanes), lanes)
        out = taps_ref[0] * ext_ref[0:nx, :, cols]
        for j in range(1, 2 * HW + 1):
            out = out + taps_ref[j] * ext_ref[j:j + nx, :, cols]
        out_ref[:, :, cols] = out
        return carry

    lax.fori_loop(0, main_ref.shape[2] // lanes, lane_chunk, 0)


def smooth_zx(raw, low, high, taps, blocks, ty=8):
    nx, ny, nz = raw.shape
    return pl.pallas_call(
        _zx_kernel,
        grid=(len(blocks),),
        in_specs=[
            pl.BlockSpec(memory_space=pltpu.SMEM),
            pl.BlockSpec((nx, ty, nz), lambda i: (0, blocks[0] + i * (blocks[-1] - blocks[0]) // max(1, len(blocks) - 1), 0)),
            pl.BlockSpec((HW, ty, nz), lambda i: (0, blocks[0] + i * (blocks[-1] - blocks[0]) // max(1, len(blocks) - 1), 0)),
            pl.BlockSpec((HW, ty, nz), lambda i: (0, blocks[0] + i * (blocks[-1] - blocks[0]) // max(1, len(blocks) - 1), 0)),
        ],
        out_specs=pl.BlockSpec((nx, ty, nz), lambda i: (0, i, 0)),
        out_shape=jax.ShapeDtypeStruct((nx, ty * len(blocks), nz), jnp.float32),
        scratch_shapes=[pltpu.VMEM((nx + 2 * HW, ty, nz), jnp.float32)],
        cost_estimate=pl.CostEstimate(
            flops=40 * nx * ty * nz * len(blocks), transcendentals=0,
            bytes_accessed=int(nx * ty * nz * len(blocks) * 10),
        ),
    )(taps, raw, low, high)


def _y_kernel(taps_ref, first_ref, middle_ref, last_ref, low_ref, high_ref, out_ref, ext_ref):
    edge = first_ref.shape[1]
    ny = middle_ref.shape[1] + 2 * edge
    ext_ref[:, HW:2 * HW] = low_ref[...]
    ext_ref[:, 2 * HW:2 * HW + edge] = first_ref[...]
    ext_ref[:, 2 * HW + edge:2 * HW + ny - edge] = middle_ref[...]
    ext_ref[:, 2 * HW + ny - edge:2 * HW + ny] = last_ref[...]
    ext_ref[:, 2 * HW + ny:3 * HW + ny] = high_ref[...]
    lanes = 128

    def lane_chunk(c, carry):
        cols = pl.ds(pl.multiple_of(c * lanes, lanes), lanes)
        out = taps_ref[0] * ext_ref[:, pl.ds(HW, ny), cols]
        for j in range(1, 2 * HW + 1):
            out = out + taps_ref[j] * ext_ref[:, pl.ds(HW + j, ny), cols]
        out_ref[:, :, cols] = out
        return carry

    lax.fori_loop(0, out_ref.shape[2] // lanes, lane_chunk, 0)


def smooth_y(edges, middle, low, high, taps, tx=8):
    nx, two_edge, nz = edges.shape
    edge = two_edge // 2
    ny = middle.shape[1] + two_edge
    return pl.pallas_call(
        _y_kernel,
        grid=(nx // tx,),
        in_specs=[
            pl.BlockSpec(memory_space=pltpu.SMEM),
            pl.BlockSpec((tx, edge, nz), lambda i: (i, 0, 0)),
            pl.BlockSpec((tx, ny - 2 * edge, nz), lambda i: (i, 0, 0)),
            pl.BlockSpec((tx, edge, nz), lambda i: (i, 1, 0)),
            pl.BlockSpec((tx, HW, nz), lambda i: (i, 0, 0)),
            pl.BlockSpec((tx, HW, nz), lambda i: (i, 0, 0)),
        ],
        out_specs=pl.BlockSpec((tx, ny, nz), lambda i: (i, 0, 0)),
        out_shape=jax.ShapeDtypeStruct((nx, ny, nz), jnp.float32),
        scratch_shapes=[pltpu.VMEM((tx, ny + 4 * HW, nz), jnp.float32)],
        cost_estimate=pl.CostEstimate(
            flops=18 * nx * ny * nz, transcendentals=0, bytes_accessed=int(nx * ny * nz * 8.8)
        ),
    )(taps, edges, middle, edges, low, high)


CHUNK = 128
HALO = 64


def halos(block, axis, dim, width):
    count = lax.axis_size(axis)
    forward = [(i, i + 1) for i in range(count - 1)]
    backward = [(target, source) for source, target in forward]
    low = lax.ppermute(
        lax.slice_in_dim(block, block.shape[dim] - width, None, axis=dim), axis, forward
    )
    high = lax.ppermute(lax.slice_in_dim(block, 0, width, axis=dim), axis, backward)
    return low, high


def extended(block, sides, width):
    for axis, dim in sides:
        count = lax.axis_size(axis)
        forward = [(i, i + 1) for i in range(count - 1)]
        backward = [(target, source) for source, target in forward]
        low = lax.ppermute(
            lax.slice_in_dim(block, block.shape[dim] - width, None, axis=dim), axis, forward
        )
        high = lax.ppermute(lax.slice_in_dim(block, 0, width, axis=dim), axis, backward)
        block = jnp.concatenate([low, block, high], axis=dim)
    return block


def band_block(values, centre):
    k = jnp.arange(CHUNK + 2 * HALO)[:, None]
    n = jnp.arange(CHUNK)[None, :]
    tap = k - n - HALO + centre
    block = jnp.zeros((CHUNK + 2 * HALO, CHUNK), jnp.float32)
    for j in range(values.shape[0]):
        block = jnp.where(tap == j, values[j], block)
    return block


def split(x):
    high = lax.reduce_precision(x, exponent_bits=8, mantissa_bits=7)
    return high.astype(jnp.bfloat16), (x - high).astype(jnp.bfloat16)


def windows(x):
    rows, length = x.shape
    chunks = length // CHUNK
    padded = jnp.pad(x, ((0, 0), (HALO, HALO)))
    pieces = padded.reshape(rows, chunks + 1, CHUNK)
    joined = jnp.concatenate([pieces[:, :chunks], pieces[:, 1:]], axis=-1)
    return joined.reshape(rows * chunks, CHUNK + 2 * HALO)


def banded(signal, block):
    rows, length = signal.shape
    x_high, x_low = split(signal)
    b_high, b_low = lax.optimization_barrier(split(block))
    w_high, w_low = windows(x_high), windows(x_low)
    out = (
        jnp.dot(w_high, b_high, preferred_element_type=jnp.float32)
        + jnp.dot(w_high, b_low, preferred_element_type=jnp.float32)
        + jnp.dot(w_low, b_high, preferred_element_type=jnp.float32)
    )
    return out.reshape(rows, length)


def filter_padded(padded, taps, axis):
    length = padded.shape[axis] - 8
    shape_out = list(padded.shape)
    shape_out[axis] = length
    result = jnp.zeros(tuple(shape_out), jnp.float32)
    for offset in range(9):
        result = result + taps[offset] * lax.slice_in_dim(
            padded, offset, offset + length, axis=axis
        )
    return result


def traverse(blocks):
    return lax.all_to_all(blocks, ("inline", "xline"), split_axis=0, concat_axis=0, tiled=True)


def local(image, weights, observed, wavelet, taps, aperture, landing):
    axes = ("inline", "xline")
    device_count = lax.axis_size("inline") * lax.axis_size("xline")
    me = lax.axis_index("inline") * lax.axis_size("xline") + lax.axis_index("xline")
    block_count, aperture_len = aperture.shape
    trace_count, samples = observed.shape
    per_block = trace_count // block_count
    rows_x, rows_y, depth_len = image.shape
    cell_count = rows_x * rows_y
    capacity = 2 * max(1, block_count * aperture_len // device_count)
    item_count = block_count * aperture_len
    tables = jnp.concatenate(
        [aperture, landing.reshape(block_count, per_block * aperture_len)], axis=1
    ).astype(jnp.float32)
    tables_all = jnp.round(lax.all_gather(tables, axes, axis=0, tiled=True))
    target_tile = aperture.reshape(item_count)
    onehot = (target_tile[:, None] == jnp.arange(device_count, dtype=jnp.int32)[None, :]).astype(
        jnp.int32
    )
    before = jnp.cumsum(onehot, axis=0) - onehot
    slot_index = jnp.sum(before * onehot, axis=1)
    target_slot = target_tile * capacity + slot_index
    item_cells = (
        landing.reshape(block_count, per_block, aperture_len)
        .transpose(0, 2, 1)
        .reshape(item_count, per_block)
    )
    cell_send = (
        jnp.zeros((device_count * capacity, per_block), jnp.int32).at[target_slot].set(item_cells)
    )
    cell_recv = lax.all_to_all(
        cell_send.reshape(device_count, capacity * per_block),
        axes,
        split_axis=0,
        concat_axis=0,
        tiled=True,
    )
    cell_recv = cell_recv.reshape(device_count * capacity * per_block)
    tile_rows = image.reshape(cell_count, depth_len)
    weight_matrix = weights.reshape(samples, depth_len)
    contract = (((1,), (1,)), ((), ()))
    half_cap = capacity // 2
    requests = cell_recv.reshape(device_count, capacity, per_block)
    returned = []
    for part in range(2):
        wanted = requests[:, part * half_cap:(part + 1) * half_cap].reshape(-1)
        predicted = lax.dot_general(
            jnp.take(tile_rows, wanted, axis=0), weight_matrix, contract,
            preferred_element_type=jnp.float32,
        ).astype(jnp.bfloat16)
        returned.append(
            traverse(predicted.reshape(device_count, half_cap * per_block, samples)).reshape(
                device_count * half_cap, per_block, samples
            )
        )
    tile_of = target_tile
    within = slot_index % half_cap
    from_first = jnp.take(returned[0], tile_of * half_cap + within, axis=0)
    from_second = jnp.take(returned[1], tile_of * half_cap + within, axis=0)
    own_preds = jnp.where(
        (slot_index < half_cap)[:, None, None], from_first, from_second
    ).reshape(block_count, aperture_len, per_block, samples)
    synthetic = jnp.sum(own_preds.astype(jnp.float32), axis=1).reshape(trace_count, samples)
    half = wavelet.shape[0] // 2
    modeled = banded(synthetic, band_block(wavelet[::-1], half))
    residual = modeled - observed.astype(jnp.float32)
    adjoint = banded(residual, band_block(wavelet, half)).astype(jnp.bfloat16)

    adjoint_all = lax.all_gather(adjoint, axes, axis=0, tiled=True)
    all_blocks = block_count * device_count
    aperture_all = tables_all[:, :aperture_len].astype(jnp.int32)
    landing_all = tables_all[:, aperture_len:].astype(jnp.int32).reshape(all_blocks * per_block, aperture_len)
    relevant = capacity * device_count
    hit = aperture_all == me
    has = jnp.any(hit, axis=1)
    entry = jnp.argmax(hit, axis=1).astype(jnp.int32)
    position = jnp.cumsum(has.astype(jnp.int32)) - 1
    slot = jnp.where(has, position, relevant)
    chosen = (
        jnp.zeros((relevant,), jnp.int32)
        .at[slot]
        .set(jnp.arange(all_blocks, dtype=jnp.int32), mode="drop")
    )
    found = jnp.sum(has.astype(jnp.int32))
    cells_all = jnp.take_along_axis(
        landing_all.reshape(all_blocks, per_block, aperture_len), entry[:, None, None], axis=2
    )[:, :, 0]
    cells = jnp.where(
        (jnp.arange(relevant) < found)[:, None], jnp.take(cells_all, chosen, axis=0), cell_count
    )
    picked = jnp.take(adjoint_all.reshape(all_blocks, per_block, samples), chosen, axis=0)
    weight_wide = jnp.pad(weight_matrix.astype(jnp.float32), ((0, 0), (HW, HW)))
    smoothed_weights = filter_padded(weight_wide, taps, 1)
    w_high, w_low = split(smoothed_weights)
    flat = picked.reshape(relevant * per_block, samples)
    per_trace = jnp.dot(flat, w_high, preferred_element_type=jnp.float32) + jnp.dot(
        flat, w_low, preferred_element_type=jnp.float32
    )
    raw_gradient = (
        jnp.zeros((cell_count, depth_len), jnp.float32)
        .at[cells.reshape(relevant * per_block)]
        .add(per_trace, mode="drop")
    )
    raw_gradient = raw_gradient.reshape(rows_x, rows_y, depth_len)
    raw_low, raw_high = halos(raw_gradient, "inline", 0, HW)
    y_blocks = rows_y // 8
    edges = smooth_zx(raw_gradient, raw_low, raw_high, taps, (0, y_blocks - 1))
    x_low, x_high = halos(edges, "xline", 1, HW)
    middle = smooth_zx(raw_gradient, raw_low, raw_high, taps, tuple(range(1, y_blocks - 1)))
    gradient = smooth_y(edges, middle, x_low, x_high, taps)
    return (gradient, residual)


def solution(mesh):
    return jax.shard_map(
        local,
        mesh=mesh,
        in_specs=(
            P("inline", "xline", None),
            P("inline", "xline", None, None),
            P(("inline", "xline"), None),
            P(),
            P(),
            P(("inline", "xline"), None),
            P(("inline", "xline"), None),
        ),
        out_specs=(P("inline", "xline", None), P(("inline", "xline"), None)),
        check_vma=False,
    )
```

```python
import jax
import jax.numpy as jnp
from jax import lax
from jax.experimental import pallas as pl
from jax.experimental.pallas import tpu as pltpu
from jax.sharding import PartitionSpec as P

HW = 4


def _zx_kernel(taps_ref, main_ref, low_ref, high_ref, out_ref, ext_ref):
    nx = main_ref.shape[0]
    ext_ref[0:HW] = low_ref[...]
    ext_ref[HW:HW + nx] = main_ref[...]
    ext_ref[HW + nx:] = high_ref[...]
    lanes = 128

    def lane_chunk(c, carry):
        cols = pl.ds(pl.multiple_of(c * lanes, lanes), lanes)
        out = taps_ref[0] * ext_ref[0:nx, :, cols]
        for j in range(1, 2 * HW + 1):
            out = out + taps_ref[j] * ext_ref[j:j + nx, :, cols]
        out_ref[:, :, cols] = out
        return carry

    lax.fori_loop(0, main_ref.shape[2] // lanes, lane_chunk, 0)


def smooth_zx(raw, low, high, taps, blocks, ty=8):
    nx, ny, nz = raw.shape
    return pl.pallas_call(
        _zx_kernel,
        grid=(len(blocks),),
        in_specs=[
            pl.BlockSpec(memory_space=pltpu.SMEM),
            pl.BlockSpec((nx, ty, nz), lambda i: (0, blocks[0] + i * (blocks[-1] - blocks[0]) // max(1, len(blocks) - 1), 0)),
            pl.BlockSpec((HW, ty, nz), lambda i: (0, blocks[0] + i * (blocks[-1] - blocks[0]) // max(1, len(blocks) - 1), 0)),
            pl.BlockSpec((HW, ty, nz), lambda i: (0, blocks[0] + i * (blocks[-1] - blocks[0]) // max(1, len(blocks) - 1), 0)),
        ],
        out_specs=pl.BlockSpec((nx, ty, nz), lambda i: (0, i, 0)),
        out_shape=jax.ShapeDtypeStruct((nx, ty * len(blocks), nz), jnp.float32),
        scratch_shapes=[pltpu.VMEM((nx + 2 * HW, ty, nz), jnp.float32)],
        cost_estimate=pl.CostEstimate(
            flops=40 * nx * ty * nz * len(blocks), transcendentals=0,
            bytes_accessed=int(nx * ty * nz * len(blocks) * 10),
        ),
    )(taps, raw, low, high)


def _y_kernel(taps_ref, first_ref, middle_ref, last_ref, low_ref, high_ref, out_ref, ext_ref):
    edge = first_ref.shape[1]
    ny = middle_ref.shape[1] + 2 * edge
    ext_ref[:, HW:2 * HW] = low_ref[...]
    ext_ref[:, 2 * HW:2 * HW + edge] = first_ref[...]
    ext_ref[:, 2 * HW + edge:2 * HW + ny - edge] = middle_ref[...]
    ext_ref[:, 2 * HW + ny - edge:2 * HW + ny] = last_ref[...]
    ext_ref[:, 2 * HW + ny:3 * HW + ny] = high_ref[...]
    lanes = 128

    def lane_chunk(c, carry):
        cols = pl.ds(pl.multiple_of(c * lanes, lanes), lanes)
        for row in range(out_ref.shape[0]):
            out = taps_ref[0] * ext_ref[row, pl.ds(HW, ny), cols]
            for j in range(1, 2 * HW + 1):
                out = out + taps_ref[j] * ext_ref[row, pl.ds(HW + j, ny), cols]
            out_ref[row, :, cols] = out
        return carry

    lax.fori_loop(0, out_ref.shape[2] // lanes, lane_chunk, 0)


def smooth_y(edges, middle, low, high, taps, tx=8):
    nx, two_edge, nz = edges.shape
    edge = two_edge // 2
    ny = middle.shape[1] + two_edge
    return pl.pallas_call(
        _y_kernel,
        grid=(nx // tx,),
        in_specs=[
            pl.BlockSpec(memory_space=pltpu.SMEM),
            pl.BlockSpec((tx, edge, nz), lambda i: (i, 0, 0)),
            pl.BlockSpec((tx, ny - 2 * edge, nz), lambda i: (i, 0, 0)),
            pl.BlockSpec((tx, edge, nz), lambda i: (i, 1, 0)),
            pl.BlockSpec((tx, HW, nz), lambda i: (i, 0, 0)),
            pl.BlockSpec((tx, HW, nz), lambda i: (i, 0, 0)),
        ],
        out_specs=pl.BlockSpec((tx, ny, nz), lambda i: (i, 0, 0)),
        out_shape=jax.ShapeDtypeStruct((nx, ny, nz), jnp.float32),
        scratch_shapes=[pltpu.VMEM((tx, ny + 4 * HW, nz), jnp.float32)],
        cost_estimate=pl.CostEstimate(
            flops=18 * nx * ny * nz, transcendentals=0, bytes_accessed=int(nx * ny * nz * 8.8)
        ),
    )(taps, edges, middle, edges, low, high)


CHUNK = 128
HALO = 64


def halos(block, axis, dim, width):
    count = lax.axis_size(axis)
    forward = [(i, i + 1) for i in range(count - 1)]
    backward = [(target, source) for source, target in forward]
    low = lax.ppermute(
        lax.slice_in_dim(block, block.shape[dim] - width, None, axis=dim), axis, forward
    )
    high = lax.ppermute(lax.slice_in_dim(block, 0, width, axis=dim), axis, backward)
    return low, high


def extended(block, sides, width):
    for axis, dim in sides:
        count = lax.axis_size(axis)
        forward = [(i, i + 1) for i in range(count - 1)]
        backward = [(target, source) for source, target in forward]
        low = lax.ppermute(
            lax.slice_in_dim(block, block.shape[dim] - width, None, axis=dim), axis, forward
        )
        high = lax.ppermute(lax.slice_in_dim(block, 0, width, axis=dim), axis, backward)
        block = jnp.concatenate([low, block, high], axis=dim)
    return block


def band_block(values, centre):
    k = jnp.arange(CHUNK + 2 * HALO)[:, None]
    n = jnp.arange(CHUNK)[None, :]
    tap = k - n - HALO + centre
    block = jnp.zeros((CHUNK + 2 * HALO, CHUNK), jnp.float32)
    for j in range(values.shape[0]):
        block = jnp.where(tap == j, values[j], block)
    return block


def split(x):
    high = lax.reduce_precision(x, exponent_bits=8, mantissa_bits=7)
    return high.astype(jnp.bfloat16), (x - high).astype(jnp.bfloat16)


def windows(x):
    rows, length = x.shape
    chunks = length // CHUNK
    padded = jnp.pad(x, ((0, 0), (HALO, HALO)))
    pieces = padded.reshape(rows, chunks + 1, CHUNK)
    joined = jnp.concatenate([pieces[:, :chunks], pieces[:, 1:]], axis=-1)
    return joined.reshape(rows * chunks, CHUNK + 2 * HALO)


def banded(signal, block):
    rows, length = signal.shape
    x_high, x_low = split(signal)
    b_high, b_low = lax.optimization_barrier(split(block))
    w_high, w_low = windows(x_high), windows(x_low)
    out = (
        jnp.dot(w_high, b_high, preferred_element_type=jnp.float32)
        + jnp.dot(w_high, b_low, preferred_element_type=jnp.float32)
        + jnp.dot(w_low, b_high, preferred_element_type=jnp.float32)
    )
    return out.reshape(rows, length)


def filter_padded(padded, taps, axis):
    length = padded.shape[axis] - 8
    shape_out = list(padded.shape)
    shape_out[axis] = length
    result = jnp.zeros(tuple(shape_out), jnp.float32)
    for offset in range(9):
        result = result + taps[offset] * lax.slice_in_dim(
            padded, offset, offset + length, axis=axis
        )
    return result


def traverse(blocks):
    return lax.all_to_all(blocks, ("inline", "xline"), split_axis=0, concat_axis=0, tiled=True)


def local(image, weights, observed, wavelet, taps, aperture, landing):
    axes = ("inline", "xline")
    device_count = lax.axis_size("inline") * lax.axis_size("xline")
    me = lax.axis_index("inline") * lax.axis_size("xline") + lax.axis_index("xline")
    block_count, aperture_len = aperture.shape
    trace_count, samples = observed.shape
    per_block = trace_count // block_count
    rows_x, rows_y, depth_len = image.shape
    cell_count = rows_x * rows_y
    capacity = 2 * max(1, block_count * aperture_len // device_count)
    item_count = block_count * aperture_len
    tables = jnp.concatenate(
        [aperture, landing.reshape(block_count, per_block * aperture_len)], axis=1
    ).astype(jnp.float32)
    tables_all = jnp.round(lax.all_gather(tables, axes, axis=0, tiled=True))
    target_tile = aperture.reshape(item_count)
    onehot = (target_tile[:, None] == jnp.arange(device_count, dtype=jnp.int32)[None, :]).astype(
        jnp.int32
    )
    before = jnp.cumsum(onehot, axis=0) - onehot
    slot_index = jnp.sum(before * onehot, axis=1)
    target_slot = target_tile * capacity + slot_index
    item_cells = (
        landing.reshape(block_count, per_block, aperture_len)
        .transpose(0, 2, 1)
        .reshape(item_count, per_block)
    )
    cell_send = (
        jnp.zeros((device_count * capacity, per_block), jnp.int32).at[target_slot].set(item_cells)
    )
    cell_recv = lax.all_to_all(
        cell_send.reshape(device_count, capacity * per_block),
        axes,
        split_axis=0,
        concat_axis=0,
        tiled=True,
    )
    cell_recv = cell_recv.reshape(device_count * capacity * per_block)
    tile_rows = image.reshape(cell_count, depth_len)
    weight_matrix = weights.reshape(samples, depth_len)
    contract = (((1,), (1,)), ((), ()))
    half_cap = capacity // 2
    requests = cell_recv.reshape(device_count, capacity, per_block)
    returned = []
    for part in range(2):
        wanted = requests[:, part * half_cap:(part + 1) * half_cap].reshape(-1)
        predicted = lax.dot_general(
            jnp.take(tile_rows, wanted, axis=0), weight_matrix, contract,
            preferred_element_type=jnp.float32,
        ).astype(jnp.bfloat16)
        returned.append(
            traverse(predicted.reshape(device_count, half_cap * per_block, samples)).reshape(
                device_count * half_cap, per_block, samples
            )
        )
    tile_of = target_tile
    within = slot_index % half_cap
    from_first = jnp.take(returned[0], tile_of * half_cap + within, axis=0)
    from_second = jnp.take(returned[1], tile_of * half_cap + within, axis=0)
    own_preds = jnp.where(
        (slot_index < half_cap)[:, None, None], from_first, from_second
    ).reshape(block_count, aperture_len, per_block, samples)
    synthetic = jnp.sum(own_preds.astype(jnp.float32), axis=1).reshape(trace_count, samples)
    half = wavelet.shape[0] // 2
    modeled = banded(synthetic, band_block(wavelet[::-1], half))
    residual = modeled - observed.astype(jnp.float32)
    adjoint = banded(residual, band_block(wavelet, half)).astype(jnp.bfloat16)

    adjoint_all = lax.all_gather(adjoint, axes, axis=0, tiled=True)
    all_blocks = block_count * device_count
    aperture_all = tables_all[:, :aperture_len].astype(jnp.int32)
    landing_all = tables_all[:, aperture_len:].astype(jnp.int32).reshape(all_blocks * per_block, aperture_len)
    relevant = capacity * device_count
    hit = aperture_all == me
    has = jnp.any(hit, axis=1)
    entry = jnp.argmax(hit, axis=1).astype(jnp.int32)
    position = jnp.cumsum(has.astype(jnp.int32)) - 1
    slot = jnp.where(has, position, relevant)
    chosen = (
        jnp.zeros((relevant,), jnp.int32)
        .at[slot]
        .set(jnp.arange(all_blocks, dtype=jnp.int32), mode="drop")
    )
    found = jnp.sum(has.astype(jnp.int32))
    cells_all = jnp.take_along_axis(
        landing_all.reshape(all_blocks, per_block, aperture_len), entry[:, None, None], axis=2
    )[:, :, 0]
    cells = jnp.where(
        (jnp.arange(relevant) < found)[:, None], jnp.take(cells_all, chosen, axis=0), cell_count
    )
    picked = jnp.take(adjoint_all.reshape(all_blocks, per_block, samples), chosen, axis=0)
    weight_wide = jnp.pad(weight_matrix.astype(jnp.float32), ((0, 0), (HW, HW)))
    smoothed_weights = filter_padded(weight_wide, taps, 1)
    w_high, w_low = split(smoothed_weights)
    flat = picked.reshape(relevant * per_block, samples)
    per_trace = jnp.dot(flat, w_high, preferred_element_type=jnp.float32) + jnp.dot(
        flat, w_low, preferred_element_type=jnp.float32
    )
    raw_gradient = (
        jnp.zeros((cell_count, depth_len), jnp.float32)
        .at[cells.reshape(relevant * per_block)]
        .add(per_trace, mode="drop")
    )
    raw_gradient = raw_gradient.reshape(rows_x, rows_y, depth_len)
    raw_low, raw_high = halos(raw_gradient, "inline", 0, HW)
    y_blocks = rows_y // 8
    edges = smooth_zx(raw_gradient, raw_low, raw_high, taps, (0, y_blocks - 1))
    x_low, x_high = halos(edges, "xline", 1, HW)
    middle = smooth_zx(raw_gradient, raw_low, raw_high, taps, tuple(range(1, y_blocks - 1)))
    gradient = smooth_y(edges, middle, x_low, x_high, taps)
    return (gradient, residual)


def solution(mesh):
    return jax.shard_map(
        local,
        mesh=mesh,
        in_specs=(
            P("inline", "xline", None),
            P("inline", "xline", None, None),
            P(("inline", "xline"), None),
            P(),
            P(),
            P(("inline", "xline"), None),
            P(("inline", "xline"), None),
        ),
        out_specs=(P("inline", "xline", None), P(("inline", "xline"), None)),
        check_vma=False,
    )
```

```python
import jax
import jax.numpy as jnp
from jax import lax
from jax.experimental import pallas as pl
from jax.experimental.pallas import tpu as pltpu
from jax.sharding import PartitionSpec as P

HW = 4


def _zx_kernel(taps_ref, main_ref, low_ref, high_ref, out_ref, ext_ref):
    nx = main_ref.shape[0]
    ext_ref[0:HW] = low_ref[...]
    ext_ref[HW:HW + nx] = main_ref[...]
    ext_ref[HW + nx:] = high_ref[...]
    lanes = 128

    def lane_chunk(c, carry):
        cols = pl.ds(pl.multiple_of(c * lanes, lanes), lanes)
        for first in range(0, nx, 8):
            out = taps_ref[0] * ext_ref[first:first + 8, :, cols]
            for j in range(1, 2 * HW + 1):
                out = out + taps_ref[j] * ext_ref[first + j:first + j + 8, :, cols]
            out_ref[first:first + 8, :, cols] = out
        return carry

    lax.fori_loop(0, main_ref.shape[2] // lanes, lane_chunk, 0)


def smooth_zx(raw, low, high, taps, blocks, ty=8):
    nx, ny, nz = raw.shape
    return pl.pallas_call(
        _zx_kernel,
        grid=(len(blocks),),
        in_specs=[
            pl.BlockSpec(memory_space=pltpu.SMEM),
            pl.BlockSpec((nx, ty, nz), lambda i: (0, blocks[0] + i * (blocks[-1] - blocks[0]) // max(1, len(blocks) - 1), 0)),
            pl.BlockSpec((HW, ty, nz), lambda i: (0, blocks[0] + i * (blocks[-1] - blocks[0]) // max(1, len(blocks) - 1), 0)),
            pl.BlockSpec((HW, ty, nz), lambda i: (0, blocks[0] + i * (blocks[-1] - blocks[0]) // max(1, len(blocks) - 1), 0)),
        ],
        out_specs=pl.BlockSpec((nx, ty, nz), lambda i: (0, i, 0)),
        out_shape=jax.ShapeDtypeStruct((nx, ty * len(blocks), nz), jnp.float32),
        scratch_shapes=[pltpu.VMEM((nx + 2 * HW, ty, nz), jnp.float32)],
        cost_estimate=pl.CostEstimate(
            flops=40 * nx * ty * nz * len(blocks), transcendentals=0,
            bytes_accessed=int(nx * ty * nz * len(blocks) * 10),
        ),
    )(taps, raw, low, high)


def _y_kernel(taps_ref, first_ref, middle_ref, last_ref, low_ref, high_ref, out_ref, ext_ref):
    edge = first_ref.shape[1]
    ny = middle_ref.shape[1] + 2 * edge
    ext_ref[:, HW:2 * HW] = low_ref[...]
    ext_ref[:, 2 * HW:2 * HW + edge] = first_ref[...]
    ext_ref[:, 2 * HW + edge:2 * HW + ny - edge] = middle_ref[...]
    ext_ref[:, 2 * HW + ny - edge:2 * HW + ny] = last_ref[...]
    ext_ref[:, 2 * HW + ny:3 * HW + ny] = high_ref[...]
    lanes = 128

    def lane_chunk(c, carry):
        cols = pl.ds(pl.multiple_of(c * lanes, lanes), lanes)
        for row in range(out_ref.shape[0]):
            out = taps_ref[0] * ext_ref[row, pl.ds(HW, ny), cols]
            for j in range(1, 2 * HW + 1):
                out = out + taps_ref[j] * ext_ref[row, pl.ds(HW + j, ny), cols]
            out_ref[row, :, cols] = out
        return carry

    lax.fori_loop(0, out_ref.shape[2] // lanes, lane_chunk, 0)


def smooth_y(edges, middle, low, high, taps, tx=8):
    nx, two_edge, nz = edges.shape
    edge = two_edge // 2
    ny = middle.shape[1] + two_edge
    return pl.pallas_call(
        _y_kernel,
        grid=(nx // tx,),
        in_specs=[
            pl.BlockSpec(memory_space=pltpu.SMEM),
            pl.BlockSpec((tx, edge, nz), lambda i: (i, 0, 0)),
            pl.BlockSpec((tx, ny - 2 * edge, nz), lambda i: (i, 0, 0)),
            pl.BlockSpec((tx, edge, nz), lambda i: (i, 1, 0)),
            pl.BlockSpec((tx, HW, nz), lambda i: (i, 0, 0)),
            pl.BlockSpec((tx, HW, nz), lambda i: (i, 0, 0)),
        ],
        out_specs=pl.BlockSpec((tx, ny, nz), lambda i: (i, 0, 0)),
        out_shape=jax.ShapeDtypeStruct((nx, ny, nz), jnp.float32),
        scratch_shapes=[pltpu.VMEM((tx, ny + 4 * HW, nz), jnp.float32)],
        cost_estimate=pl.CostEstimate(
            flops=18 * nx * ny * nz, transcendentals=0, bytes_accessed=int(nx * ny * nz * 8.8)
        ),
    )(taps, edges, middle, edges, low, high)


CHUNK = 128
HALO = 64


def halos(block, axis, dim, width):
    count = lax.axis_size(axis)
    forward = [(i, i + 1) for i in range(count - 1)]
    backward = [(target, source) for source, target in forward]
    low = lax.ppermute(
        lax.slice_in_dim(block, block.shape[dim] - width, None, axis=dim), axis, forward
    )
    high = lax.ppermute(lax.slice_in_dim(block, 0, width, axis=dim), axis, backward)
    return low, high


def extended(block, sides, width):
    for axis, dim in sides:
        count = lax.axis_size(axis)
        forward = [(i, i + 1) for i in range(count - 1)]
        backward = [(target, source) for source, target in forward]
        low = lax.ppermute(
            lax.slice_in_dim(block, block.shape[dim] - width, None, axis=dim), axis, forward
        )
        high = lax.ppermute(lax.slice_in_dim(block, 0, width, axis=dim), axis, backward)
        block = jnp.concatenate([low, block, high], axis=dim)
    return block


def band_block(values, centre):
    k = jnp.arange(CHUNK + 2 * HALO)[:, None]
    n = jnp.arange(CHUNK)[None, :]
    tap = k - n - HALO + centre
    block = jnp.zeros((CHUNK + 2 * HALO, CHUNK), jnp.float32)
    for j in range(values.shape[0]):
        block = jnp.where(tap == j, values[j], block)
    return block


def split(x):
    high = lax.reduce_precision(x, exponent_bits=8, mantissa_bits=7)
    return high.astype(jnp.bfloat16), (x - high).astype(jnp.bfloat16)


def windows(x):
    rows, length = x.shape
    chunks = length // CHUNK
    padded = jnp.pad(x, ((0, 0), (HALO, HALO)))
    pieces = padded.reshape(rows, chunks + 1, CHUNK)
    joined = jnp.concatenate([pieces[:, :chunks], pieces[:, 1:]], axis=-1)
    return joined.reshape(rows * chunks, CHUNK + 2 * HALO)


def banded(signal, block):
    rows, length = signal.shape
    x_high, x_low = split(signal)
    b_high, b_low = lax.optimization_barrier(split(block))
    w_high, w_low = windows(x_high), windows(x_low)
    out = (
        jnp.dot(w_high, b_high, preferred_element_type=jnp.float32)
        + jnp.dot(w_high, b_low, preferred_element_type=jnp.float32)
        + jnp.dot(w_low, b_high, preferred_element_type=jnp.float32)
    )
    return out.reshape(rows, length)


def filter_padded(padded, taps, axis):
    length = padded.shape[axis] - 8
    shape_out = list(padded.shape)
    shape_out[axis] = length
    result = jnp.zeros(tuple(shape_out), jnp.float32)
    for offset in range(9):
        result = result + taps[offset] * lax.slice_in_dim(
            padded, offset, offset + length, axis=axis
        )
    return result


def traverse(blocks):
    return lax.all_to_all(blocks, ("inline", "xline"), split_axis=0, concat_axis=0, tiled=True)


def local(image, weights, observed, wavelet, taps, aperture, landing):
    axes = ("inline", "xline")
    device_count = lax.axis_size("inline") * lax.axis_size("xline")
    me = lax.axis_index("inline") * lax.axis_size("xline") + lax.axis_index("xline")
    block_count, aperture_len = aperture.shape
    trace_count, samples = observed.shape
    per_block = trace_count // block_count
    rows_x, rows_y, depth_len = image.shape
    cell_count = rows_x * rows_y
    capacity = 2 * max(1, block_count * aperture_len // device_count)
    item_count = block_count * aperture_len
    tables = jnp.concatenate(
        [aperture, landing.reshape(block_count, per_block * aperture_len)], axis=1
    ).astype(jnp.float32)
    tables_all = jnp.round(lax.all_gather(tables, axes, axis=0, tiled=True))
    target_tile = aperture.reshape(item_count)
    onehot = (target_tile[:, None] == jnp.arange(device_count, dtype=jnp.int32)[None, :]).astype(
        jnp.int32
    )
    before = jnp.cumsum(onehot, axis=0) - onehot
    slot_index = jnp.sum(before * onehot, axis=1)
    target_slot = target_tile * capacity + slot_index
    item_cells = (
        landing.reshape(block_count, per_block, aperture_len)
        .transpose(0, 2, 1)
        .reshape(item_count, per_block)
    )
    cell_send = (
        jnp.zeros((device_count * capacity, per_block), jnp.int32).at[target_slot].set(item_cells)
    )
    cell_recv = lax.all_to_all(
        cell_send.reshape(device_count, capacity * per_block),
        axes,
        split_axis=0,
        concat_axis=0,
        tiled=True,
    )
    cell_recv = cell_recv.reshape(device_count * capacity * per_block)
    tile_rows = image.reshape(cell_count, depth_len)
    weight_matrix = weights.reshape(samples, depth_len)
    contract = (((1,), (1,)), ((), ()))
    half_cap = capacity // 2
    requests = cell_recv.reshape(device_count, capacity, per_block)
    returned = []
    for part in range(2):
        wanted = requests[:, part * half_cap:(part + 1) * half_cap].reshape(-1)
        predicted = lax.dot_general(
            jnp.take(tile_rows, wanted, axis=0), weight_matrix, contract,
            preferred_element_type=jnp.float32,
        ).astype(jnp.bfloat16)
        returned.append(
            traverse(predicted.reshape(device_count, half_cap * per_block, samples)).reshape(
                device_count * half_cap, per_block, samples
            )
        )
    tile_of = target_tile
    within = slot_index % half_cap
    from_first = jnp.take(returned[0], tile_of * half_cap + within, axis=0)
    from_second = jnp.take(returned[1], tile_of * half_cap + within, axis=0)
    own_preds = jnp.where(
        (slot_index < half_cap)[:, None, None], from_first, from_second
    ).reshape(block_count, aperture_len, per_block, samples)
    synthetic = jnp.sum(own_preds.astype(jnp.float32), axis=1).reshape(trace_count, samples)
    half = wavelet.shape[0] // 2
    modeled = banded(synthetic, band_block(wavelet[::-1], half))
    residual = modeled - observed.astype(jnp.float32)
    adjoint = banded(residual, band_block(wavelet, half)).astype(jnp.bfloat16)

    adjoint_all = lax.all_gather(adjoint, axes, axis=0, tiled=True)
    all_blocks = block_count * device_count
    aperture_all = tables_all[:, :aperture_len].astype(jnp.int32)
    landing_all = tables_all[:, aperture_len:].astype(jnp.int32).reshape(all_blocks * per_block, aperture_len)
    relevant = capacity * device_count
    hit = aperture_all == me
    has = jnp.any(hit, axis=1)
    entry = jnp.argmax(hit, axis=1).astype(jnp.int32)
    position = jnp.cumsum(has.astype(jnp.int32)) - 1
    slot = jnp.where(has, position, relevant)
    chosen = (
        jnp.zeros((relevant,), jnp.int32)
        .at[slot]
        .set(jnp.arange(all_blocks, dtype=jnp.int32), mode="drop")
    )
    found = jnp.sum(has.astype(jnp.int32))
    cells_all = jnp.take_along_axis(
        landing_all.reshape(all_blocks, per_block, aperture_len), entry[:, None, None], axis=2
    )[:, :, 0]
    cells = jnp.where(
        (jnp.arange(relevant) < found)[:, None], jnp.take(cells_all, chosen, axis=0), cell_count
    )
    picked = jnp.take(adjoint_all.reshape(all_blocks, per_block, samples), chosen, axis=0)
    weight_wide = jnp.pad(weight_matrix.astype(jnp.float32), ((0, 0), (HW, HW)))
    smoothed_weights = filter_padded(weight_wide, taps, 1)
    w_high, w_low = split(smoothed_weights)
    flat = picked.reshape(relevant * per_block, samples)
    per_trace = jnp.dot(flat, w_high, preferred_element_type=jnp.float32) + jnp.dot(
        flat, w_low, preferred_element_type=jnp.float32
    )
    raw_gradient = (
        jnp.zeros((cell_count, depth_len), jnp.float32)
        .at[cells.reshape(relevant * per_block)]
        .add(per_trace, mode="drop")
    )
    raw_gradient = raw_gradient.reshape(rows_x, rows_y, depth_len)
    raw_low, raw_high = halos(raw_gradient, "inline", 0, HW)
    y_blocks = rows_y // 8
    edges = smooth_zx(raw_gradient, raw_low, raw_high, taps, (0, y_blocks - 1))
    x_low, x_high = halos(edges, "xline", 1, HW)
    middle = smooth_zx(raw_gradient, raw_low, raw_high, taps, tuple(range(1, y_blocks - 1)))
    gradient = smooth_y(edges, middle, x_low, x_high, taps)
    return (gradient, residual)


def solution(mesh):
    return jax.shard_map(
        local,
        mesh=mesh,
        in_specs=(
            P("inline", "xline", None),
            P("inline", "xline", None, None),
            P(("inline", "xline"), None),
            P(),
            P(),
            P(("inline", "xline"), None),
            P(("inline", "xline"), None),
        ),
        out_specs=(P("inline", "xline", None), P(("inline", "xline"), None)),
        check_vma=False,
    )
```
